32 devices in a mesh: energy: 4 (over z), momentum: 4 (over x, core), space: 2 (over y).
Axes of the slice: x: 2, y: 2, z: 4, core: 2. Of those that a mesh axis runs over, the one named last changes fastest.
Arguments:
- blocks: float32 [8, 4, 2, 2, 256, 256], P('energy', 'momentum', 'space'), may hold values from -0.1 to 1.1
- inverse_guess: float32 [8, 4, 2, 2, 256, 256], P('energy', 'momentum', 'space'), may hold values from -1.8 to 2.4, as said below
- coupling: float32 [4, 2, 2, 128, 128], P('momentum', 'space'), may hold values from -0.37625 to 0.37625
- pair_index: int32 [2, 128], P('space'), may hold values from 0 to 255, as said below
- phonon_shift: int32 [8], replicated, may hold values from 1 to 8, as said below
- phonon_strength: float32 [2, 8, 4], replicated, may hold values from 0.05 to 0.5
- momentum_table: int32 [4, 4], replicated, may hold values from 0 to 3, as said below
Outputs:
- green: float32 [8, 4, 2, 2, 256, 256], P('energy', 'momentum', 'space')
- self_energy: float32 [8, 4, 2, 128, 512], P('energy', 'momentum', 'space')
The draws below stay inside these ranges and needn't reach their ends.
Inputs may be any that keep to these rules, and one draw needn't show every extreme that they name: `inverse_guess`: an approximate inverse of the matching block of blocks. `pair_index`: in each block s, entries 8 a to 8 a + 7 are a 16 + b for 8 distinct atoms b, the first of them b = a. `phonon_shift`: one entry equals 8 and another equals 1. `momentum_table`: each row and each column holds every momentum once.
All inputs are finite; a program needn't handle non-finite values.
Results may differ from the reference program's by a relative error of at most 0.0001.
Values sent between devices are 32-bit elements; how exact they have to be, the bound alone decides.
No kernel may reach another device: no remote copies, remote signals or barrier semaphores. Data moves between devices by JAX's collectives and lax.ppermute only.
A program may use at most 128 MiB of HBM per device.

```python
import math
import jax
import jax.numpy as jnp
from jax import lax

B = 256
ORB = 16
ATOMS = 16
NBR = 8
NP = 128
NB = 128
NW = 8
SHIFT_MAX = 8
NEWTON = 2
NE = 8
NK = 4
NSB = 2


def draw_operator_pair(key):
    base_key = jax.random.fold_in(key, 101)
    first_key, second_key = jax.random.split(base_key)
    diagonal = jax.random.uniform(first_key, (NE, NK, NSB, B), jnp.float32, 0.5, 1.0)
    spread_scale = 0.2 / (2.0 * math.sqrt(2.0 * B))
    disorder = spread_scale * jax.random.truncated_normal(second_key, -6.0, 6.0, (NE, NK, NSB, 2, B, B), jnp.float32)
    identity = jnp.eye(B, dtype=jnp.float32)
    row_ids = jnp.arange(B, dtype=jnp.int32)[:, None]
    col_ids = jnp.arange(B, dtype=jnp.int32)[None, :]
    forward = (col_ids == row_ids + (B - NB)) & (row_ids < NB)
    backward = (row_ids == col_ids + (B - NB)) & (col_ids < NB)
    link = 0.4 * (forward | backward).astype(jnp.float32)
    inverse = 1.0 / diagonal
    real_part = diagonal[..., :, None] * identity + disorder[..., 0, :, :]
    imag_part = link + disorder[..., 1, :, :]
    blocks = jnp.stack([real_part, imag_part], axis=3)
    outer = inverse[..., :, None] * inverse[..., None, :]
    approx_real = inverse[..., :, None] * identity - outer * disorder[..., 0, :, :]
    approx_imag = -outer * imag_part
    approximate = jnp.stack([approx_real, approx_imag], axis=3)
    return (blocks, approximate)


def draw_blocks(key, part):
    return draw_operator_pair(key)[0]


def draw_inverse_guess(key, part):
    return draw_operator_pair(key)[1]


def draw_coupling(key, part):
    base_key = jax.random.fold_in(key, 503)
    first_key, second_key = jax.random.split(base_key)
    phases = jax.random.uniform(first_key, (NK, NSB, NB), jnp.float32, -math.pi, math.pi)
    noise_scale = 0.07 / math.sqrt(2.0 * NB)
    noise = noise_scale * jax.random.truncated_normal(second_key, -6.0, 6.0, (NK, NSB, 2, NB, NB), jnp.float32)
    identity = jnp.eye(NB, dtype=jnp.float32)
    diagonal_part = 0.35 * jnp.stack([jnp.cos(phases)[..., :, None] * identity, jnp.sin(phases)[..., :, None] * identity], axis=2)
    return diagonal_part + noise


def draw_pair_index(key, part):
    base_key = jax.random.fold_in(key, 203)
    block_keys = jax.random.split(base_key, NSB)

    def one_block(block_key):
        atom_keys = jax.random.split(block_key, ATOMS)
        offsets = jax.vmap(lambda atom_key: jax.random.permutation(atom_key, ATOMS - 1)[:NBR - 1] + 1)(atom_keys)
        offsets = jnp.concatenate([jnp.zeros((ATOMS, 1), jnp.int32), offsets.astype(jnp.int32)], axis=1)
        atom_ids = jnp.arange(ATOMS, dtype=jnp.int32)[:, None]
        partner = (atom_ids + offsets) % ATOMS
        return (atom_ids * ATOMS + partner).reshape(NP)
    return jax.vmap(one_block)(block_keys).astype(jnp.int32)


def draw_phonon_shift(key, part):
    base_key = jax.random.fold_in(key, 307)
    first_key, second_key = jax.random.split(base_key)
    offsets = jax.random.randint(first_key, (NW,), 1, SHIFT_MAX + 1)
    special = jax.random.randint(second_key, (), 0, NW)
    slots = jnp.arange(NW)
    offsets = jnp.where(slots == (special + 1) % NW, 1, offsets)
    return jnp.where(slots == special, SHIFT_MAX, offsets).astype(jnp.int32)


def draw_momentum_table(key, part):
    base_key = jax.random.fold_in(key, 409)
    first_key, second_key = jax.random.split(base_key)
    first_order = jax.random.permutation(first_key, NK)
    second_order = jax.random.permutation(second_key, NK)
    return ((first_order[:, None] - second_order[None, :]) % NK).astype(jnp.int32)


def setup_inputs(seed: int = 0) -> dict:
    arg_keys = jax.random.split(jax.random.key(seed), 8)
    return {
        "blocks": draw_blocks(jax.random.fold_in(arg_keys[7], 71), 0),
        "inverse_guess": draw_inverse_guess(jax.random.fold_in(arg_keys[7], 71), 0),
        "coupling": draw_coupling(jax.random.fold_in(arg_keys[7], 71), 0),
        "pair_index": draw_pair_index(jax.random.fold_in(arg_keys[7], 71), 0),
        "phonon_shift": draw_phonon_shift(jax.random.fold_in(arg_keys[7], 71), 0),
        "phonon_strength": jnp.clip(jnp.exp(jax.random.uniform(arg_keys[5], (2, NW, NK), jnp.float32, math.log(0.05), math.log(0.5))), 0.05, 0.5),
        "momentum_table": draw_momentum_table(jax.random.fold_in(arg_keys[7], 71), 0),
    }


HIGHEST = lax.Precision.HIGHEST


def complex_product(first_factor, second_factor):
    real_part = jnp.matmul(first_factor[..., 0, :, :], second_factor[..., 0, :, :], precision=HIGHEST) - jnp.matmul(first_factor[..., 1, :, :], second_factor[..., 1, :, :], precision=HIGHEST)
    imag_part = jnp.matmul(first_factor[..., 0, :, :], second_factor[..., 1, :, :], precision=HIGHEST) + jnp.matmul(first_factor[..., 1, :, :], second_factor[..., 0, :, :], precision=HIGHEST)
    return jnp.stack([real_part, imag_part], axis=-3)


def refine(blocks, approximate, coupling_block, incoming):
    adjoint = jnp.stack([jnp.swapaxes(coupling_block[..., 0, :, :], -1, -2), -jnp.swapaxes(coupling_block[..., 1, :, :], -1, -2)], axis=-3)
    schur_term = complex_product(complex_product(adjoint, incoming), coupling_block)
    edge_size = incoming.shape[-1]
    system = blocks.at[..., :edge_size, :edge_size].add(-schur_term)
    for newton_step in range(NEWTON):
        approximate = 2.0 * approximate - complex_product(approximate, complex_product(system, approximate))
    return approximate, approximate[..., -edge_size:, -edge_size:]


def phonon_matrix(phonon_shift, phonon_strength, momentum_table, energies):
    momenta = momentum_table.shape[0]
    chosen = (momentum_table[:, :, None] == jnp.arange(momenta, dtype=jnp.int32)[None, None, :]).astype(jnp.float32)
    momentum_mix = jnp.einsum('kqj,dwq->kjdw', chosen, phonon_strength, precision=HIGHEST)
    energy_rows = jnp.arange(energies, dtype=jnp.int32)
    energy_gap = energy_rows[None, :] - energy_rows[:, None]
    emission = (energy_gap[None, :, :] == -phonon_shift[:, None, None]).astype(jnp.float32)
    absorption = (energy_gap[None, :, :] == phonon_shift[:, None, None]).astype(jnp.float32)
    shift_table = jnp.stack([emission, absorption], axis=0)
    return jnp.einsum('kjdw,dwEF->kjEF', momentum_mix, shift_table, precision=HIGHEST)


def reference(blocks, inverse_guess, coupling, pair_index, phonon_shift, phonon_strength, momentum_table):
    boundary = jnp.zeros((NE, NK, 2, NB, NB), jnp.float32)
    collected = []
    for space_block in range(NSB):
        green_block, boundary = refine(blocks[:, :, space_block], inverse_guess[:, :, space_block], coupling[None, :, space_block], boundary)
        collected.append(green_block)
    green = jnp.stack(collected, axis=2)
    atom_tiles = green.reshape(NE, NK, NSB, 2, ATOMS, ORB, ATOMS, ORB).transpose(0, 1, 2, 4, 6, 3, 5, 7).reshape(NE, NK, NSB, ATOMS * ATOMS, 2 * ORB * ORB)
    picked = jnp.take_along_axis(atom_tiles, pair_index[None, None, :, :, None], axis=3)
    mixing = phonon_matrix(phonon_shift, phonon_strength, momentum_table, NE)
    self_energy = jnp.einsum('kjEF,Fjspx->Ekspx', mixing, picked, precision=HIGHEST)
    return green, self_energy
```

```python
import jax
import jax.numpy as jnp
from jax import lax
from jax.sharding import PartitionSpec as P

ORB = 16
ATOMS = 16
NEWTON = 2


HIGHEST = lax.Precision.HIGHEST
NEWTON_PRECISION = lax.Precision.HIGHEST


def from_behind(shard, axis, by):
    count = lax.axis_size(axis)
    pairs = [(i, i + by) for i in range(count) if 0 <= i + by < count]
    return lax.ppermute(shard, axis, pairs)


def complex_product(first_factor, second_factor, precision=HIGHEST):
    real_part = jnp.matmul(
        first_factor[..., 0, :, :], second_factor[..., 0, :, :], precision=precision
    ) - jnp.matmul(first_factor[..., 1, :, :], second_factor[..., 1, :, :], precision=precision)
    imag_part = jnp.matmul(
        first_factor[..., 0, :, :], second_factor[..., 1, :, :], precision=precision
    ) + jnp.matmul(first_factor[..., 1, :, :], second_factor[..., 0, :, :], precision=precision)
    return jnp.stack([real_part, imag_part], axis=-3)


def newton_product(first_factor, second_factor):
    return complex_product(first_factor, second_factor, NEWTON_PRECISION)


def adjoint_of(coupling_block):
    return jnp.stack(
        [
            jnp.swapaxes(coupling_block[..., 0, :, :], -1, -2),
            -jnp.swapaxes(coupling_block[..., 1, :, :], -1, -2),
        ],
        axis=-3,
    )


def schur_of(adjoint, coupling_block, incoming):
    return complex_product(complex_product(adjoint, incoming), coupling_block)


def sweep(blocks, guess, coupling_block):
    space_count = lax.axis_size("space")
    size = blocks.shape[-1]
    edge = coupling_block.shape[-1]
    lead = slice(0, edge)
    trail = slice(size - edge, size)
    adjoint = adjoint_of(coupling_block)

    first = 2.0 * guess - newton_product(guess, newton_product(blocks, guess))
    left = guess[..., :, lead]
    right = guess[..., lead, :]

    applied_trail = newton_product(blocks, first[..., :, trail])
    boundary = 2.0 * first[..., trail, trail] - newton_product(
        first[..., trail, :], applied_trail
    )
    applied_left = newton_product(blocks, left)

    for section in range(1, space_count - 1):
        incoming = from_behind(boundary, "space", 1)
        schur = schur_of(adjoint, coupling_block, incoming)
        mixed = newton_product(schur, right)
        step_trail = first[..., :, trail] + newton_product(left, mixed[..., :, trail])
        step_rows = first[..., trail, :] + newton_product(left[..., trail, :], mixed)
        system_trail = applied_trail + newton_product(applied_left, mixed[..., :, trail])
        system_trail = system_trail.at[..., lead, :].add(
            -newton_product(schur, step_trail[..., lead, :])
        )
        boundary = 2.0 * step_trail[..., trail, :] - newton_product(step_rows, system_trail)

    applied = newton_product(blocks, first)
    if space_count > 1:
        incoming = from_behind(boundary, "space", 1)
        schur = schur_of(adjoint, coupling_block, incoming)
        mixed = newton_product(schur, right)
        step = first + newton_product(left, mixed)
        system_step = applied + newton_product(applied_left, mixed)
        system_step = system_step.at[..., lead, :].add(
            -newton_product(schur, step[..., lead, :])
        )
    else:
        step = first
        system_step = applied
    return 2.0 * step - newton_product(step, system_step)


def phonon_matrix(phonon_shift, phonon_strength, momentum_table, energies):
    momenta = momentum_table.shape[0]
    chosen = (
        momentum_table[:, :, None] == jnp.arange(momenta, dtype=jnp.int32)[None, None, :]
    ).astype(jnp.float32)
    momentum_mix = jnp.einsum("kqj,dwq->kjdw", chosen, phonon_strength, precision=HIGHEST)
    energy_rows = jnp.arange(energies, dtype=jnp.int32)
    energy_gap = energy_rows[None, :] - energy_rows[:, None]
    emission = (energy_gap[None, :, :] == -phonon_shift[:, None, None]).astype(jnp.float32)
    absorption = (energy_gap[None, :, :] == phonon_shift[:, None, None]).astype(jnp.float32)
    shift_table = jnp.stack([emission, absorption], axis=0)
    return jnp.einsum("kjdw,dwEF->kjEF", momentum_mix, shift_table, precision=HIGHEST)


def body(
    blocks, inverse_guess, coupling, pair_index, phonon_shift, phonon_strength, momentum_table
):
    local_blocks = blocks[:, 0, 0]
    local_guess = inverse_guess[:, 0, 0]
    coupling_block = coupling[0, 0]
    energy_count = local_blocks.shape[0]
    green_block = sweep(local_blocks, local_guess, coupling_block)
    atom_tiles = (
        green_block.reshape(energy_count, 2, ATOMS, ORB, ATOMS, ORB)
        .transpose(0, 2, 4, 1, 3, 5)
        .reshape(energy_count, ATOMS * ATOMS, 2 * ORB * ORB)
    )
    picked = jnp.take(atom_tiles, pair_index[0], axis=1)[:, None, None]
    momenta = momentum_table.shape[0]
    energy_groups = lax.axis_size("energy")
    mixing = phonon_matrix(
        phonon_shift, phonon_strength, momentum_table, energy_count * energy_groups
    )
    by_pairs = lax.all_to_all(
        picked, ("energy", "momentum"), split_axis=3, concat_axis=1, tiled=True
    )
    pair_count = by_pairs.shape[3]
    arranged = by_pairs.reshape(energy_count, energy_groups, momenta, pair_count, by_pairs.shape[4])
    mixing_grid = mixing.reshape(
        momenta, momenta, energy_groups, energy_count, energy_groups, energy_count
    )
    summed = jnp.einsum("kjabcd,dcjpx->bakpx", mixing_grid, arranged, precision=HIGHEST)
    summed = summed.reshape(energy_count, energy_groups * momenta, 1, pair_count, by_pairs.shape[4])
    self_energy = lax.all_to_all(
        summed, ("energy", "momentum"), split_axis=1, concat_axis=3, tiled=True
    )
    return (green_block[:, None, None], self_energy)


def solution(mesh):
    return jax.shard_map(
        body,
        mesh=mesh,
        in_specs=(
            P("energy", "momentum", "space", None, None, None),
            P("energy", "momentum", "space", None, None, None),
            P("momentum", "space", None, None, None),
            P("space", None),
            P(),
            P(),
            P(),
        ),
        out_specs=(
            P("energy", "momentum", "space", None, None, None),
            P("energy", "momentum", "space", None, None),
        ),
        check_vma=False,
    )
```

```python
import jax
import jax.numpy as jnp
from jax import lax
from jax.sharding import PartitionSpec as P

ORB = 16
ATOMS = 16
NEWTON = 2


HIGHEST = lax.Precision.HIGHEST
NEWTON_PRECISION = lax.Precision.HIGHEST


def from_behind(shard, axis, by):
    count = lax.axis_size(axis)
    pairs = [(i, i + by) for i in range(count) if 0 <= i + by < count]
    return lax.ppermute(shard, axis, pairs)


def complex_product(first_factor, second_factor, precision=HIGHEST):
    first_real, first_imag = first_factor
    second_real, second_imag = second_factor
    real_part = jnp.matmul(first_real, second_real, precision=precision) - jnp.matmul(
        first_imag, second_imag, precision=precision
    )
    imag_part = jnp.matmul(first_real, second_imag, precision=precision) + jnp.matmul(
        first_imag, second_real, precision=precision
    )
    return (real_part, imag_part)


def newton_product(first_factor, second_factor):
    return complex_product(first_factor, second_factor, NEWTON_PRECISION)


def part(pair, rows=slice(None), cols=slice(None)):
    return tuple(value[..., rows, cols] for value in pair)


def combine(first_weight, first, second):
    return tuple(first_weight * a - b for a, b in zip(first, second))


def add(first, second):
    return tuple(a + b for a, b in zip(first, second))


def sweep(blocks, guess, coupling_block):
    space_count = lax.axis_size("space")
    size = blocks[0].shape[-1]
    edge = coupling_block[0].shape[-1]
    lead = slice(0, edge)
    trail = slice(size - edge, size)
    adjoint = (jnp.swapaxes(coupling_block[0], -1, -2), -jnp.swapaxes(coupling_block[1], -1, -2))

    def schur_of(incoming):
        return complex_product(complex_product(adjoint, incoming), coupling_block)

    def lead_rows_minus(values, schur, rows):
        update = newton_product(schur, rows)
        return tuple(v.at[..., lead, :].add(-u) for v, u in zip(values, update))

    first = combine(2.0, guess, newton_product(guess, newton_product(blocks, guess)))
    left = part(guess, cols=lead)
    right = part(guess, rows=lead)

    applied_trail = newton_product(blocks, part(first, cols=trail))
    boundary = combine(
        2.0, part(first, trail, trail), newton_product(part(first, rows=trail), applied_trail)
    )
    applied_left = newton_product(blocks, left)

    for section in range(1, space_count - 1):
        incoming = from_behind(boundary, "space", 1)
        schur = schur_of(incoming)
        mixed = newton_product(schur, right)
        mixed_trail = part(mixed, cols=trail)
        step_trail = add(part(first, cols=trail), newton_product(left, mixed_trail))
        step_rows = add(part(first, rows=trail), newton_product(part(left, rows=trail), mixed))
        system_trail = add(applied_trail, newton_product(applied_left, mixed_trail))
        system_trail = lead_rows_minus(system_trail, schur, part(step_trail, rows=lead))
        boundary = combine(
            2.0, part(step_trail, rows=trail), newton_product(step_rows, system_trail)
        )

    applied = newton_product(blocks, first)
    if space_count > 1:
        incoming = from_behind(boundary, "space", 1)
        schur = schur_of(incoming)
        mixed = newton_product(schur, right)
        step = add(first, newton_product(left, mixed))
        system_step = add(applied, newton_product(applied_left, mixed))
        system_step = lead_rows_minus(system_step, schur, part(step, rows=lead))
    else:
        step = first
        system_step = applied
    return combine(2.0, step, newton_product(step, system_step))


def phonon_matrix(phonon_shift, phonon_strength, momentum_table, energies):
    momenta = momentum_table.shape[0]
    chosen = (
        momentum_table[:, :, None] == jnp.arange(momenta, dtype=jnp.int32)[None, None, :]
    ).astype(jnp.float32)
    momentum_mix = jnp.einsum("kqj,dwq->kjdw", chosen, phonon_strength, precision=HIGHEST)
    energy_rows = jnp.arange(energies, dtype=jnp.int32)
    energy_gap = energy_rows[None, :] - energy_rows[:, None]
    emission = (energy_gap[None, :, :] == -phonon_shift[:, None, None]).astype(jnp.float32)
    absorption = (energy_gap[None, :, :] == phonon_shift[:, None, None]).astype(jnp.float32)
    shift_table = jnp.stack([emission, absorption], axis=0)
    return jnp.einsum("kjdw,dwEF->kjEF", momentum_mix, shift_table, precision=HIGHEST)


def pick_tiles(green_pair, pair_index):
    energy_count = green_pair[0].shape[0]
    partner = (pair_index % ATOMS).reshape(ATOMS, -1)
    per_atom = partner.shape[1]
    picked = []
    for values in green_pair:
        tiles = values.reshape(energy_count, ATOMS, ORB, ATOMS, ORB)
        chosen = jnp.take_along_axis(tiles, partner[None, :, None, :, None], axis=3)
        picked.append(chosen.transpose(0, 1, 3, 2, 4))
    picked = jnp.stack(picked, axis=3)
    return picked.reshape(energy_count, ATOMS * per_atom, 2 * ORB * ORB)


def body(
    blocks, inverse_guess, coupling, pair_index, phonon_shift, phonon_strength, momentum_table
):
    local_blocks = (blocks[:, 0, 0, 0], blocks[:, 0, 0, 1])
    local_guess = (inverse_guess[:, 0, 0, 0], inverse_guess[:, 0, 0, 1])
    coupling_block = (coupling[0, 0, 0], coupling[0, 0, 1])
    energy_count = blocks.shape[0]
    green_pair = sweep(local_blocks, local_guess, coupling_block)
    green_block = jnp.stack(green_pair, axis=1)
    picked = pick_tiles(green_pair, pair_index[0])[:, None, None]
    momenta = momentum_table.shape[0]
    energy_groups = lax.axis_size("energy")
    mixing = phonon_matrix(
        phonon_shift, phonon_strength, momentum_table, energy_count * energy_groups
    )
    by_pairs = lax.all_to_all(
        picked, ("energy", "momentum"), split_axis=3, concat_axis=1, tiled=True
    )
    pair_count = by_pairs.shape[3]
    arranged = by_pairs.reshape(energy_count, energy_groups, momenta, pair_count, by_pairs.shape[4])
    mixing_grid = mixing.reshape(
        momenta, momenta, energy_groups, energy_count, energy_groups, energy_count
    )
    summed = jnp.einsum("kjabcd,dcjpx->bakpx", mixing_grid, arranged, precision=HIGHEST)
    summed = summed.reshape(energy_count, energy_groups * momenta, 1, pair_count, by_pairs.shape[4])
    self_energy = lax.all_to_all(
        summed, ("energy", "momentum"), split_axis=1, concat_axis=3, tiled=True
    )
    return (green_block[:, None, None], self_energy)


def solution(mesh):
    return jax.shard_map(
        body,
        mesh=mesh,
        in_specs=(
            P("energy", "momentum", "space", None, None, None),
            P("energy", "momentum", "space", None, None, None),
            P("momentum", "space", None, None, None),
            P("space", None),
            P(),
            P(),
            P(),
        ),
        out_specs=(
            P("energy", "momentum", "space", None, None, None),
            P("energy", "momentum", "space", None, None),
        ),
        check_vma=False,
    )
```

```python
import jax
import jax.numpy as jnp
from jax import lax
from jax.sharding import PartitionSpec as P
from jax.experimental import pallas as pl
from jax.experimental.pallas import tpu as pltpu

ORB = 16
ATOMS = 16
NEWTON = 2


HIGHEST = lax.Precision.HIGHEST
NEWTON_PRECISION = lax.Precision.HIGHEST


def from_behind(shard, axis, by):
    count = lax.axis_size(axis)
    pairs = [(i, i + by) for i in range(count) if 0 <= i + by < count]
    return lax.ppermute(shard, axis, pairs)


def complex_product(first_factor, second_factor, precision=HIGHEST):
    first_real, first_imag = first_factor
    second_real, second_imag = second_factor
    real_part = jnp.matmul(first_real, second_real, precision=precision) - jnp.matmul(
        first_imag, second_imag, precision=precision
    )
    imag_part = jnp.matmul(first_real, second_imag, precision=precision) + jnp.matmul(
        first_imag, second_real, precision=precision
    )
    return (real_part, imag_part)


def newton_product(first_factor, second_factor):
    return complex_product(first_factor, second_factor, NEWTON_PRECISION)


def part(pair, rows=slice(None), cols=slice(None)):
    return tuple(value[..., rows, cols] for value in pair)


def combine(first_weight, first, second):
    return tuple(first_weight * a - b for a, b in zip(first, second))


def add(first, second):
    return tuple(a + b for a, b in zip(first, second))


def sweep(blocks, guess, coupling_block):
    space_count = lax.axis_size("space")
    size = blocks[0].shape[-1]
    edge = coupling_block[0].shape[-1]
    lead = slice(0, edge)
    trail = slice(size - edge, size)
    adjoint = (jnp.swapaxes(coupling_block[0], -1, -2), -jnp.swapaxes(coupling_block[1], -1, -2))

    def schur_of(incoming):
        return complex_product(complex_product(adjoint, incoming), coupling_block)

    def lead_rows_minus(values, schur, rows):
        update = newton_product(schur, rows)
        return tuple(v.at[..., lead, :].add(-u) for v, u in zip(values, update))

    first = combine(2.0, guess, newton_product(guess, newton_product(blocks, guess)))
    left = part(guess, cols=lead)
    right = part(guess, rows=lead)

    applied_trail = newton_product(blocks, part(first, cols=trail))
    boundary = combine(
        2.0, part(first, trail, trail), newton_product(part(first, rows=trail), applied_trail)
    )
    applied_left = newton_product(blocks, left)

    for section in range(1, space_count - 1):
        incoming = from_behind(boundary, "space", 1)
        schur = schur_of(incoming)
        mixed = newton_product(schur, right)
        mixed_trail = part(mixed, cols=trail)
        step_trail = add(part(first, cols=trail), newton_product(left, mixed_trail))
        step_rows = add(part(first, rows=trail), newton_product(part(left, rows=trail), mixed))
        system_trail = add(applied_trail, newton_product(applied_left, mixed_trail))
        system_trail = lead_rows_minus(system_trail, schur, part(step_trail, rows=lead))
        boundary = combine(
            2.0, part(step_trail, rows=trail), newton_product(step_rows, system_trail)
        )

    applied = newton_product(blocks, first)
    if space_count > 1:
        incoming = from_behind(boundary, "space", 1)
        schur = schur_of(incoming)
        mixed = newton_product(schur, right)
        step = add(first, newton_product(left, mixed))
        system_step = add(applied, newton_product(applied_left, mixed))
        system_step = lead_rows_minus(system_step, schur, part(step, rows=lead))
    else:
        step = first
        system_step = applied
    return combine(2.0, step, newton_product(step, system_step))


def phonon_matrix(phonon_shift, phonon_strength, momentum_table, energies):
    momenta = momentum_table.shape[0]
    chosen = (
        momentum_table[:, :, None] == jnp.arange(momenta, dtype=jnp.int32)[None, None, :]
    ).astype(jnp.float32)
    momentum_mix = jnp.einsum("kqj,dwq->kjdw", chosen, phonon_strength, precision=HIGHEST)
    energy_rows = jnp.arange(energies, dtype=jnp.int32)
    energy_gap = energy_rows[None, :] - energy_rows[:, None]
    emission = (energy_gap[None, :, :] == -phonon_shift[:, None, None]).astype(jnp.float32)
    absorption = (energy_gap[None, :, :] == phonon_shift[:, None, None]).astype(jnp.float32)
    shift_table = jnp.stack([emission, absorption], axis=0)
    return jnp.einsum("kjdw,dwEF->kjEF", momentum_mix, shift_table, precision=HIGHEST)


def pick_kernel(partner_ref, real_ref, imag_ref, out_ref):
    energy_count, size, _ = real_ref.shape
    atoms = size // ORB
    per_atom = partner_ref.shape[0] // atoms
    width = per_atom * ORB
    groups = 2 * energy_count
    rows = groups * ORB
    flat = ORB * ORB

    spread_rows = lax.broadcasted_iota(jnp.int32, (width, flat), 0)
    spread_cols = lax.broadcasted_iota(jnp.int32, (width, flat), 1)
    spread = (spread_rows % ORB == spread_cols % ORB).astype(jnp.float32)
    keep_rows = lax.broadcasted_iota(jnp.int32, (per_atom * rows, flat), 0)
    keep_cols = lax.broadcasted_iota(jnp.int32, (per_atom * rows, flat), 1)
    keep = keep_rows % ORB == keep_cols // ORB
    total_rows = lax.broadcasted_iota(jnp.int32, (groups * per_atom, per_atom * rows), 0)
    total_cols = lax.broadcasted_iota(jnp.int32, (groups * per_atom, per_atom * rows), 1)
    total = (
        (total_cols // rows == total_rows % per_atom)
        & ((total_cols // ORB) % groups == total_rows // per_atom)
    ).astype(jnp.float32)
    lane_tile = lax.broadcasted_iota(jnp.int32, (rows, width), 1) // ORB
    pick_rows = lax.broadcasted_iota(jnp.int32, (size, width), 0)
    pick_cols = lax.broadcasted_iota(jnp.int32, (size, width), 1)

    def one_atom(atom, carry):
        target = jnp.zeros((size, width), jnp.int32)
        for j in range(per_atom):
            target = jnp.where(pick_cols // ORB == j, partner_ref[atom * per_atom + j], target)
        pick = (
            (pick_rows // ORB == target) & (pick_rows % ORB == pick_cols % ORB)
        ).astype(jnp.float32)
        start = pl.multiple_of(atom * ORB, ORB)
        stripes = []
        for e in range(energy_count):
            stripes.append(real_ref[e, pl.ds(start, ORB), :])
            stripes.append(imag_ref[e, pl.ds(start, ORB), :])
        stripes = jnp.concatenate(stripes, axis=0)
        chosen = jnp.dot(stripes, pick, precision=HIGHEST, preferred_element_type=jnp.float32)
        masked = jnp.concatenate(
            [jnp.where(lane_tile == j, chosen, 0.0) for j in range(per_atom)], axis=0
        )
        spread_out = jnp.dot(masked, spread, precision=HIGHEST, preferred_element_type=jnp.float32)
        spread_out = jnp.where(keep, spread_out, 0.0)
        summed = jnp.dot(total, spread_out, precision=HIGHEST, preferred_element_type=jnp.float32)
        out_start = pl.multiple_of(atom * per_atom, per_atom)
        for e in range(energy_count):
            for component in range(2):
                g = 2 * e + component
                out_ref[e, pl.ds(out_start, per_atom), pl.ds(component * flat, flat)] = summed[
                    g * per_atom : (g + 1) * per_atom, :
                ]
        return carry

    lax.fori_loop(0, atoms, one_atom, 0)


def pick_tiles(green_pair, pair_index):
    energy_count = green_pair[0].shape[0]
    pair_count = pair_index.shape[0]
    partner = pair_index % ATOMS
    return pl.pallas_call(
        pick_kernel,
        out_shape=jax.ShapeDtypeStruct((energy_count, pair_count, 2 * ORB * ORB), jnp.float32),
        in_specs=[
            pl.BlockSpec(memory_space=pltpu.SMEM),
            pl.BlockSpec(memory_space=pltpu.VMEM),
            pl.BlockSpec(memory_space=pltpu.VMEM),
        ],
        out_specs=pl.BlockSpec(memory_space=pltpu.VMEM),
    )(partner, green_pair[0], green_pair[1])


def body(
    blocks, inverse_guess, coupling, pair_index, phonon_shift, phonon_strength, momentum_table
):
    local_blocks = (blocks[:, 0, 0, 0], blocks[:, 0, 0, 1])
    local_guess = (inverse_guess[:, 0, 0, 0], inverse_guess[:, 0, 0, 1])
    coupling_block = (coupling[0, 0, 0], coupling[0, 0, 1])
    energy_count = blocks.shape[0]
    green_pair = sweep(local_blocks, local_guess, coupling_block)
    green_block = jnp.stack(green_pair, axis=1)
    picked = pick_tiles(green_pair, pair_index[0])[:, None, None]
    momenta = momentum_table.shape[0]
    energy_groups = lax.axis_size("energy")
    mixing = phonon_matrix(
        phonon_shift, phonon_strength, momentum_table, energy_count * energy_groups
    )
    by_pairs = lax.all_to_all(
        picked, ("energy", "momentum"), split_axis=3, concat_axis=1, tiled=True
    )
    pair_count = by_pairs.shape[3]
    arranged = by_pairs.reshape(energy_count, energy_groups, momenta, pair_count, by_pairs.shape[4])
    mixing_grid = mixing.reshape(
        momenta, momenta, energy_groups, energy_count, energy_groups, energy_count
    )
    summed = jnp.einsum("kjabcd,dcjpx->bakpx", mixing_grid, arranged, precision=HIGHEST)
    summed = summed.reshape(energy_count, energy_groups * momenta, 1, pair_count, by_pairs.shape[4])
    self_energy = lax.all_to_all(
        summed, ("energy", "momentum"), split_axis=1, concat_axis=3, tiled=True
    )
    return (green_block[:, None, None], self_energy)


def solution(mesh):
    return jax.shard_map(
        body,
        mesh=mesh,
        in_specs=(
            P("energy", "momentum", "space", None, None, None),
            P("energy", "momentum", "space", None, None, None),
            P("momentum", "space", None, None, None),
            P("space", None),
            P(),
            P(),
            P(),
        ),
        out_specs=(
            P("energy", "momentum", "space", None, None, None),
            P("energy", "momentum", "space", None, None),
        ),
        check_vma=False,
    )
```

```python
import jax
import jax.numpy as jnp
from jax import lax
from jax.sharding import PartitionSpec as P
from jax.experimental import pallas as pl
from jax.experimental.pallas import tpu as pltpu

ORB = 16
ATOMS = 16
NEWTON = 2


HIGHEST = lax.Precision.HIGHEST
NEWTON_PRECISION = lax.Precision.HIGH


def from_behind(shard, axis, by):
    count = lax.axis_size(axis)
    pairs = [(i, i + by) for i in range(count) if 0 <= i + by < count]
    return lax.ppermute(shard, axis, pairs)


def complex_product(first_factor, second_factor, precision=HIGHEST):
    first_real, first_imag = first_factor
    second_real, second_imag = second_factor
    real_part = jnp.matmul(first_real, second_real, precision=precision) - jnp.matmul(
        first_imag, second_imag, precision=precision
    )
    imag_part = jnp.matmul(first_real, second_imag, precision=precision) + jnp.matmul(
        first_imag, second_real, precision=precision
    )
    return (real_part, imag_part)


def newton_product(first_factor, second_factor):
    return complex_product(first_factor, second_factor, NEWTON_PRECISION)


def part(pair, rows=slice(None), cols=slice(None)):
    return tuple(value[..., rows, cols] for value in pair)


def combine(first_weight, first, second):
    return tuple(first_weight * a - b for a, b in zip(first, second))


def add(first, second):
    return tuple(a + b for a, b in zip(first, second))


def sweep(blocks, guess, coupling_block):
    space_count = lax.axis_size("space")
    size = blocks[0].shape[-1]
    edge = coupling_block[0].shape[-1]
    lead = slice(0, edge)
    trail = slice(size - edge, size)
    adjoint = (jnp.swapaxes(coupling_block[0], -1, -2), -jnp.swapaxes(coupling_block[1], -1, -2))

    def schur_of(incoming):
        return complex_product(complex_product(adjoint, incoming), coupling_block)

    def lead_rows_minus(values, schur, rows):
        update = newton_product(schur, rows)
        return tuple(v.at[..., lead, :].add(-u) for v, u in zip(values, update))

    first = combine(2.0, guess, newton_product(guess, newton_product(blocks, guess)))
    left = part(guess, cols=lead)
    right = part(guess, rows=lead)

    applied_trail = newton_product(blocks, part(first, cols=trail))
    boundary = combine(
        2.0, part(first, trail, trail), newton_product(part(first, rows=trail), applied_trail)
    )
    applied_left = newton_product(blocks, left)

    for section in range(1, space_count - 1):
        incoming = from_behind(boundary, "space", 1)
        schur = schur_of(incoming)
        mixed = newton_product(schur, right)
        mixed_trail = part(mixed, cols=trail)
        step_trail = add(part(first, cols=trail), newton_product(left, mixed_trail))
        step_rows = add(part(first, rows=trail), newton_product(part(left, rows=trail), mixed))
        system_trail = add(applied_trail, newton_product(applied_left, mixed_trail))
        system_trail = lead_rows_minus(system_trail, schur, part(step_trail, rows=lead))
        boundary = combine(
            2.0, part(step_trail, rows=trail), newton_product(step_rows, system_trail)
        )

    applied = newton_product(blocks, first)
    if space_count > 1:
        incoming = from_behind(boundary, "space", 1)
        schur = schur_of(incoming)
        mixed = newton_product(schur, right)
        step = add(first, newton_product(left, mixed))
        system_step = add(applied, newton_product(applied_left, mixed))
        system_step = lead_rows_minus(system_step, schur, part(step, rows=lead))
    else:
        step = first
        system_step = applied
    return combine(2.0, step, newton_product(step, system_step))


def phonon_matrix(phonon_shift, phonon_strength, momentum_table, energies):
    momenta = momentum_table.shape[0]
    chosen = (
        momentum_table[:, :, None] == jnp.arange(momenta, dtype=jnp.int32)[None, None, :]
    ).astype(jnp.float32)
    momentum_mix = jnp.einsum("kqj,dwq->kjdw", chosen, phonon_strength, precision=HIGHEST)
    energy_rows = jnp.arange(energies, dtype=jnp.int32)
    energy_gap = energy_rows[None, :] - energy_rows[:, None]
    emission = (energy_gap[None, :, :] == -phonon_shift[:, None, None]).astype(jnp.float32)
    absorption = (energy_gap[None, :, :] == phonon_shift[:, None, None]).astype(jnp.float32)
    shift_table = jnp.stack([emission, absorption], axis=0)
    return jnp.einsum("kjdw,dwEF->kjEF", momentum_mix, shift_table, precision=HIGHEST)


def pick_kernel(partner_ref, real_ref, imag_ref, out_ref):
    energy_count, size, _ = real_ref.shape
    atoms = size // ORB
    per_atom = partner_ref.shape[0] // atoms
    width = per_atom * ORB
    groups = 2 * energy_count
    rows = groups * ORB
    flat = ORB * ORB

    spread_rows = lax.broadcasted_iota(jnp.int32, (width, flat), 0)
    spread_cols = lax.broadcasted_iota(jnp.int32, (width, flat), 1)
    spread = (spread_rows % ORB == spread_cols % ORB).astype(jnp.float32)
    keep_rows = lax.broadcasted_iota(jnp.int32, (per_atom * rows, flat), 0)
    keep_cols = lax.broadcasted_iota(jnp.int32, (per_atom * rows, flat), 1)
    keep = keep_rows % ORB == keep_cols // ORB
    total_rows = lax.broadcasted_iota(jnp.int32, (groups * per_atom, per_atom * rows), 0)
    total_cols = lax.broadcasted_iota(jnp.int32, (groups * per_atom, per_atom * rows), 1)
    total = (
        (total_cols // rows == total_rows % per_atom)
        & ((total_cols // ORB) % groups == total_rows // per_atom)
    ).astype(jnp.float32)
    lane_tile = lax.broadcasted_iota(jnp.int32, (rows, width), 1) // ORB
    pick_rows = lax.broadcasted_iota(jnp.int32, (size, width), 0)
    pick_cols = lax.broadcasted_iota(jnp.int32, (size, width), 1)

    def one_atom(atom, carry):
        target = jnp.zeros((size, width), jnp.int32)
        for j in range(per_atom):
            target = jnp.where(pick_cols // ORB == j, partner_ref[atom * per_atom + j], target)
        pick = (
            (pick_rows // ORB == target) & (pick_rows % ORB == pick_cols % ORB)
        ).astype(jnp.float32)
        start = pl.multiple_of(atom * ORB, ORB)
        stripes = []
        for e in range(energy_count):
            stripes.append(real_ref[e, pl.ds(start, ORB), :])
            stripes.append(imag_ref[e, pl.ds(start, ORB), :])
        stripes = jnp.concatenate(stripes, axis=0)
        chosen = jnp.dot(stripes, pick, precision=HIGHEST, preferred_element_type=jnp.float32)
        masked = jnp.concatenate(
            [jnp.where(lane_tile == j, chosen, 0.0) for j in range(per_atom)], axis=0
        )
        spread_out = jnp.dot(masked, spread, precision=HIGHEST, preferred_element_type=jnp.float32)
        spread_out = jnp.where(keep, spread_out, 0.0)
        summed = jnp.dot(total, spread_out, precision=HIGHEST, preferred_element_type=jnp.float32)
        out_start = pl.multiple_of(atom * per_atom, per_atom)
        for e in range(energy_count):
            for component in range(2):
                g = 2 * e + component
                out_ref[e, pl.ds(out_start, per_atom), pl.ds(component * flat, flat)] = summed[
                    g * per_atom : (g + 1) * per_atom, :
                ]
        return carry

    lax.fori_loop(0, atoms, one_atom, 0)


def pick_tiles(green_pair, pair_index):
    energy_count = green_pair[0].shape[0]
    pair_count = pair_index.shape[0]
    partner = pair_index % ATOMS
    return pl.pallas_call(
        pick_kernel,
        out_shape=jax.ShapeDtypeStruct((energy_count, pair_count, 2 * ORB * ORB), jnp.float32),
        in_specs=[
            pl.BlockSpec(memory_space=pltpu.SMEM),
            pl.BlockSpec(memory_space=pltpu.VMEM),
            pl.BlockSpec(memory_space=pltpu.VMEM),
        ],
        out_specs=pl.BlockSpec(memory_space=pltpu.VMEM),
    )(partner, green_pair[0], green_pair[1])


def body(
    blocks, inverse_guess, coupling, pair_index, phonon_shift, phonon_strength, momentum_table
):
    local_blocks = (blocks[:, 0, 0, 0], blocks[:, 0, 0, 1])
    local_guess = (inverse_guess[:, 0, 0, 0], inverse_guess[:, 0, 0, 1])
    coupling_block = (coupling[0, 0, 0], coupling[0, 0, 1])
    energy_count = blocks.shape[0]
    green_pair = sweep(local_blocks, local_guess, coupling_block)
    green_block = jnp.stack(green_pair, axis=1)
    picked = pick_tiles(green_pair, pair_index[0])[:, None, None]
    momenta = momentum_table.shape[0]
    energy_groups = lax.axis_size("energy")
    mixing = phonon_matrix(
        phonon_shift, phonon_strength, momentum_table, energy_count * energy_groups
    )
    by_pairs = lax.all_to_all(
        picked, ("energy", "momentum"), split_axis=3, concat_axis=1, tiled=True
    )
    pair_count = by_pairs.shape[3]
    arranged = by_pairs.reshape(energy_count, energy_groups, momenta, pair_count, by_pairs.shape[4])
    mixing_grid = mixing.reshape(
        momenta, momenta, energy_groups, energy_count, energy_groups, energy_count
    )
    summed = jnp.einsum("kjabcd,dcjpx->bakpx", mixing_grid, arranged, precision=HIGHEST)
    summed = summed.reshape(energy_count, energy_groups * momenta, 1, pair_count, by_pairs.shape[4])
    self_energy = lax.all_to_all(
        summed, ("energy", "momentum"), split_axis=1, concat_axis=3, tiled=True
    )
    return (green_block[:, None, None], self_energy)


def solution(mesh):
    return jax.shard_map(
        body,
        mesh=mesh,
        in_specs=(
            P("energy", "momentum", "space", None, None, None),
            P("energy", "momentum", "space", None, None, None),
            P("momentum", "space", None, None, None),
            P("space", None),
            P(),
            P(),
            P(),
        ),
        out_specs=(
            P("energy", "momentum", "space", None, None, None),
            P("energy", "momentum", "space", None, None),
        ),
        check_vma=False,
    )
```

```python
import jax
import jax.numpy as jnp
from jax import lax
from jax.sharding import PartitionSpec as P
from jax.experimental import pallas as pl
from jax.experimental.pallas import tpu as pltpu

ORB = 16
ATOMS = 16
NEWTON = 2


HIGHEST = lax.Precision.HIGHEST
FIRST_STEP_PRECISION = lax.Precision.HIGH


def from_behind(shard, axis, by):
    count = lax.axis_size(axis)
    pairs = [(i, i + by) for i in range(count) if 0 <= i + by < count]
    return lax.ppermute(shard, axis, pairs)


def complex_product(first_factor, second_factor, precision=HIGHEST):
    first_real, first_imag = first_factor
    second_real, second_imag = second_factor
    real_part = jnp.matmul(first_real, second_real, precision=precision) - jnp.matmul(
        first_imag, second_imag, precision=precision
    )
    imag_part = jnp.matmul(first_real, second_imag, precision=precision) + jnp.matmul(
        first_imag, second_real, precision=precision
    )
    return (real_part, imag_part)


def newton_product(first_factor, second_factor):
    return complex_product(first_factor, second_factor, HIGHEST)


def first_step_product(first_factor, second_factor):
    return complex_product(first_factor, second_factor, FIRST_STEP_PRECISION)


def part(pair, rows=slice(None), cols=slice(None)):
    return tuple(value[..., rows, cols] for value in pair)


def combine(first_weight, first, second):
    return tuple(first_weight * a - b for a, b in zip(first, second))


def add(first, second):
    return tuple(a + b for a, b in zip(first, second))


def sweep(blocks, guess, coupling_block):
    space_count = lax.axis_size("space")
    size = blocks[0].shape[-1]
    edge = coupling_block[0].shape[-1]
    lead = slice(0, edge)
    trail = slice(size - edge, size)
    adjoint = (jnp.swapaxes(coupling_block[0], -1, -2), -jnp.swapaxes(coupling_block[1], -1, -2))

    def schur_of(incoming):
        return complex_product(complex_product(adjoint, incoming), coupling_block)

    def lead_rows_minus(values, schur, rows):
        update = newton_product(schur, rows)
        return tuple(v.at[..., lead, :].add(-u) for v, u in zip(values, update))

    first = combine(2.0, guess, first_step_product(guess, first_step_product(blocks, guess)))
    left = part(guess, cols=lead)
    right = part(guess, rows=lead)

    applied_trail = newton_product(blocks, part(first, cols=trail))
    boundary = combine(
        2.0, part(first, trail, trail), newton_product(part(first, rows=trail), applied_trail)
    )
    applied_left = newton_product(blocks, left)

    for section in range(1, space_count - 1):
        incoming = from_behind(boundary, "space", 1)
        schur = schur_of(incoming)
        mixed = first_step_product(schur, right)
        mixed_trail = part(mixed, cols=trail)
        step_trail = add(part(first, cols=trail), newton_product(left, mixed_trail))
        step_rows = add(part(first, rows=trail), newton_product(part(left, rows=trail), mixed))
        system_trail = add(applied_trail, newton_product(applied_left, mixed_trail))
        system_trail = lead_rows_minus(system_trail, schur, part(step_trail, rows=lead))
        boundary = combine(
            2.0, part(step_trail, rows=trail), newton_product(step_rows, system_trail)
        )

    applied = newton_product(blocks, first)
    if space_count > 1:
        incoming = from_behind(boundary, "space", 1)
        schur = schur_of(incoming)
        mixed = first_step_product(schur, right)
        step = add(first, newton_product(left, mixed))
        system_step = add(applied, newton_product(applied_left, mixed))
        system_step = lead_rows_minus(system_step, schur, part(step, rows=lead))
    else:
        step = first
        system_step = applied
    return combine(2.0, step, newton_product(step, system_step))


def phonon_matrix(phonon_shift, phonon_strength, momentum_table, energies):
    momenta = momentum_table.shape[0]
    chosen = (
        momentum_table[:, :, None] == jnp.arange(momenta, dtype=jnp.int32)[None, None, :]
    ).astype(jnp.float32)
    momentum_mix = jnp.einsum("kqj,dwq->kjdw", chosen, phonon_strength, precision=HIGHEST)
    energy_rows = jnp.arange(energies, dtype=jnp.int32)
    energy_gap = energy_rows[None, :] - energy_rows[:, None]
    emission = (energy_gap[None, :, :] == -phonon_shift[:, None, None]).astype(jnp.float32)
    absorption = (energy_gap[None, :, :] == phonon_shift[:, None, None]).astype(jnp.float32)
    shift_table = jnp.stack([emission, absorption], axis=0)
    return jnp.einsum("kjdw,dwEF->kjEF", momentum_mix, shift_table, precision=HIGHEST)


def pick_kernel(partner_ref, real_ref, imag_ref, out_ref):
    energy_count, size, _ = real_ref.shape
    atoms = size // ORB
    per_atom = partner_ref.shape[0] // atoms
    width = per_atom * ORB
    groups = 2 * energy_count
    rows = groups * ORB
    flat = ORB * ORB

    spread_rows = lax.broadcasted_iota(jnp.int32, (width, flat), 0)
    spread_cols = lax.broadcasted_iota(jnp.int32, (width, flat), 1)
    spread = (spread_rows % ORB == spread_cols % ORB).astype(jnp.float32)
    keep_rows = lax.broadcasted_iota(jnp.int32, (per_atom * rows, flat), 0)
    keep_cols = lax.broadcasted_iota(jnp.int32, (per_atom * rows, flat), 1)
    keep = keep_rows % ORB == keep_cols // ORB
    total_rows = lax.broadcasted_iota(jnp.int32, (groups * per_atom, per_atom * rows), 0)
    total_cols = lax.broadcasted_iota(jnp.int32, (groups * per_atom, per_atom * rows), 1)
    total = (
        (total_cols // rows == total_rows % per_atom)
        & ((total_cols // ORB) % groups == total_rows // per_atom)
    ).astype(jnp.float32)
    lane_tile = lax.broadcasted_iota(jnp.int32, (rows, width), 1) // ORB
    pick_rows = lax.broadcasted_iota(jnp.int32, (size, width), 0)
    pick_cols = lax.broadcasted_iota(jnp.int32, (size, width), 1)

    def one_atom(atom, carry):
        target = jnp.zeros((size, width), jnp.int32)
        for j in range(per_atom):
            target = jnp.where(pick_cols // ORB == j, partner_ref[atom * per_atom + j], target)
        pick = (
            (pick_rows // ORB == target) & (pick_rows % ORB == pick_cols % ORB)
        ).astype(jnp.float32)
        start = pl.multiple_of(atom * ORB, ORB)
        stripes = []
        for e in range(energy_count):
            stripes.append(real_ref[e, pl.ds(start, ORB), :])
            stripes.append(imag_ref[e, pl.ds(start, ORB), :])
        stripes = jnp.concatenate(stripes, axis=0)
        chosen = jnp.dot(stripes, pick, precision=HIGHEST, preferred_element_type=jnp.float32)
        masked = jnp.concatenate(
            [jnp.where(lane_tile == j, chosen, 0.0) for j in range(per_atom)], axis=0
        )
        spread_out = jnp.dot(masked, spread, precision=HIGHEST, preferred_element_type=jnp.float32)
        spread_out = jnp.where(keep, spread_out, 0.0)
        summed = jnp.dot(total, spread_out, precision=HIGHEST, preferred_element_type=jnp.float32)
        out_start = pl.multiple_of(atom * per_atom, per_atom)
        for e in range(energy_count):
            for component in range(2):
                g = 2 * e + component
                out_ref[e, pl.ds(out_start, per_atom), pl.ds(component * flat, flat)] = summed[
                    g * per_atom : (g + 1) * per_atom, :
                ]
        return carry

    lax.fori_loop(0, atoms, one_atom, 0)


def pick_tiles(green_pair, pair_index):
    energy_count = green_pair[0].shape[0]
    pair_count = pair_index.shape[0]
    partner = pair_index % ATOMS
    return pl.pallas_call(
        pick_kernel,
        out_shape=jax.ShapeDtypeStruct((energy_count, pair_count, 2 * ORB * ORB), jnp.float32),
        in_specs=[
            pl.BlockSpec(memory_space=pltpu.SMEM),
            pl.BlockSpec(memory_space=pltpu.VMEM),
            pl.BlockSpec(memory_space=pltpu.VMEM),
        ],
        out_specs=pl.BlockSpec(memory_space=pltpu.VMEM),
    )(partner, green_pair[0], green_pair[1])


def body(
    blocks, inverse_guess, coupling, pair_index, phonon_shift, phonon_strength, momentum_table
):
    local_blocks = (blocks[:, 0, 0, 0], blocks[:, 0, 0, 1])
    local_guess = (inverse_guess[:, 0, 0, 0], inverse_guess[:, 0, 0, 1])
    coupling_block = (coupling[0, 0, 0], coupling[0, 0, 1])
    energy_count = blocks.shape[0]
    green_pair = sweep(local_blocks, local_guess, coupling_block)
    green_block = jnp.stack(green_pair, axis=1)
    picked = pick_tiles(green_pair, pair_index[0])[:, None, None]
    momenta = momentum_table.shape[0]
    energy_groups = lax.axis_size("energy")
    mixing = phonon_matrix(
        phonon_shift, phonon_strength, momentum_table, energy_count * energy_groups
    )
    by_pairs = lax.all_to_all(
        picked, ("energy", "momentum"), split_axis=3, concat_axis=1, tiled=True
    )
    pair_count = by_pairs.shape[3]
    arranged = by_pairs.reshape(energy_count, energy_groups, momenta, pair_count, by_pairs.shape[4])
    mixing_grid = mixing.reshape(
        momenta, momenta, energy_groups, energy_count, energy_groups, energy_count
    )
    summed = jnp.einsum("kjabcd,dcjpx->bakpx", mixing_grid, arranged, precision=HIGHEST)
    summed = summed.reshape(energy_count, energy_groups * momenta, 1, pair_count, by_pairs.shape[4])
    self_energy = lax.all_to_all(
        summed, ("energy", "momentum"), split_axis=1, concat_axis=3, tiled=True
    )
    return (green_block[:, None, None], self_energy)


def solution(mesh):
    return jax.shard_map(
        body,
        mesh=mesh,
        in_specs=(
            P("energy", "momentum", "space", None, None, None),
            P("energy", "momentum", "space", None, None, None),
            P("momentum", "space", None, None, None),
            P("space", None),
            P(),
            P(),
            P(),
        ),
        out_specs=(
            P("energy", "momentum", "space", None, None, None),
            P("energy", "momentum", "space", None, None),
        ),
        check_vma=False,
    )
```

```python
import jax
import jax.numpy as jnp
from jax import lax
from jax.sharding import PartitionSpec as P
from jax.experimental import pallas as pl
from jax.experimental.pallas import tpu as pltpu

ORB = 16
ATOMS = 16
NEWTON = 2


HIGHEST = lax.Precision.HIGHEST
FIRST_STEP_PRECISION = lax.Precision.HIGHEST


def from_behind(shard, axis, by):
    count = lax.axis_size(axis)
    pairs = [(i, i + by) for i in range(count) if 0 <= i + by < count]
    return lax.ppermute(shard, axis, pairs)


def complex_product(first_factor, second_factor, precision=HIGHEST):
    first_real, first_imag = first_factor
    second_real, second_imag = second_factor
    real_part = jnp.matmul(first_real, second_real, precision=precision) - jnp.matmul(
        first_imag, second_imag, precision=precision
    )
    imag_part = jnp.matmul(first_real, second_imag, precision=precision) + jnp.matmul(
        first_imag, second_real, precision=precision
    )
    return (real_part, imag_part)


def newton_product(first_factor, second_factor):
    return complex_product(first_factor, second_factor, HIGHEST)


def first_step_product(first_factor, second_factor):
    return complex_product(first_factor, second_factor, FIRST_STEP_PRECISION)


def part(pair, rows=slice(None), cols=slice(None)):
    return tuple(value[..., rows, cols] for value in pair)


def combine(first_weight, first, second):
    return tuple(first_weight * a - b for a, b in zip(first, second))


def add(first, second):
    return tuple(a + b for a, b in zip(first, second))


def sweep(blocks, guess, coupling_block):
    space_count = lax.axis_size("space")
    size = blocks[0].shape[-1]
    edge = coupling_block[0].shape[-1]
    lead = slice(0, edge)
    trail = slice(size - edge, size)
    adjoint = (jnp.swapaxes(coupling_block[0], -1, -2), -jnp.swapaxes(coupling_block[1], -1, -2))

    def schur_of(incoming):
        return complex_product(complex_product(adjoint, incoming), coupling_block)

    def lead_rows_minus(values, schur, rows):
        update = newton_product(schur, rows)
        return tuple(v.at[..., lead, :].add(-u) for v, u in zip(values, update))

    first = combine(2.0, guess, first_step_product(guess, first_step_product(blocks, guess)))
    left = part(guess, cols=lead)
    right = part(guess, rows=lead)

    applied_trail = newton_product(blocks, part(first, cols=trail))
    boundary = combine(
        2.0, part(first, trail, trail), newton_product(part(first, rows=trail), applied_trail)
    )
    applied_left = newton_product(blocks, left)

    for section in range(1, space_count - 1):
        incoming = from_behind(boundary, "space", 1)
        schur = schur_of(incoming)
        mixed = first_step_product(schur, right)
        mixed_trail = part(mixed, cols=trail)
        step_trail = add(part(first, cols=trail), newton_product(left, mixed_trail))
        step_rows = add(part(first, rows=trail), newton_product(part(left, rows=trail), mixed))
        system_trail = add(applied_trail, newton_product(applied_left, mixed_trail))
        system_trail = lead_rows_minus(system_trail, schur, part(step_trail, rows=lead))
        boundary = combine(
            2.0, part(step_trail, rows=trail), newton_product(step_rows, system_trail)
        )

    applied = newton_product(blocks, first)
    if space_count > 1:
        incoming = from_behind(boundary, "space", 1)
        schur = schur_of(incoming)
        mixed = first_step_product(schur, right)
        step = add(first, newton_product(left, mixed))
        system_step = add(applied, newton_product(applied_left, mixed))
        system_step = lead_rows_minus(system_step, schur, part(step, rows=lead))
    else:
        step = first
        system_step = applied
    return combine(2.0, step, newton_product(step, system_step))


def phonon_matrix(phonon_shift, phonon_strength, momentum_table, energies):
    momenta = momentum_table.shape[0]
    chosen = (
        momentum_table[:, :, None] == jnp.arange(momenta, dtype=jnp.int32)[None, None, :]
    ).astype(jnp.float32)
    momentum_mix = jnp.einsum("kqj,dwq->kjdw", chosen, phonon_strength, precision=HIGHEST)
    energy_rows = jnp.arange(energies, dtype=jnp.int32)
    energy_gap = energy_rows[None, :] - energy_rows[:, None]
    emission = (energy_gap[None, :, :] == -phonon_shift[:, None, None]).astype(jnp.float32)
    absorption = (energy_gap[None, :, :] == phonon_shift[:, None, None]).astype(jnp.float32)
    shift_table = jnp.stack([emission, absorption], axis=0)
    return jnp.einsum("kjdw,dwEF->kjEF", momentum_mix, shift_table, precision=HIGHEST)


def pick_kernel(target_ref, real_ref, imag_ref, out_ref):
    energy_count, size, _ = real_ref.shape
    atoms, width = target_ref.shape
    per_atom = width // ORB
    sublanes = 8
    flat = ORB * ORB
    halves = ORB // sublanes

    pick_rows = lax.broadcasted_iota(jnp.int32, (size, width), 0)
    pick_cols = lax.broadcasted_iota(jnp.int32, (size, width), 1)
    row_atom = pick_rows // ORB
    same_orbital = pick_rows % ORB == pick_cols % ORB
    grid_rows = lax.broadcasted_iota(jnp.int32, (sublanes, width), 0)
    grid_cols = lax.broadcasted_iota(jnp.int32, (sublanes, width), 1) // ORB
    diagonal = [(grid_cols - grid_rows) % per_atom == d for d in range(per_atom)]

    def one_atom(atom, carry):
        target = target_ref[pl.ds(atom, 1), :]
        pick = jnp.where((row_atom == target) & same_orbital, 1.0, 0.0)
        start = pl.multiple_of(atom * ORB, ORB)
        stripes = []
        for e in range(energy_count):
            stripes.append(real_ref[e, pl.ds(start, ORB), :])
            stripes.append(imag_ref[e, pl.ds(start, ORB), :])
        stripes = jnp.concatenate(stripes, axis=0)
        chosen = jnp.dot(stripes, pick, precision=HIGHEST, preferred_element_type=jnp.float32)
        out_start = pl.multiple_of(atom * per_atom, per_atom)
        for g in range(2 * energy_count):
            for half in range(halves):
                row = g * ORB + half * sublanes
                grid = chosen[row : row + sublanes, :]
                flipped = grid
                for d in range(1, per_atom):
                    moved = pltpu.roll(grid, (sublanes - d) % sublanes, 0)
                    moved = pltpu.roll(moved, d * ORB, 1)
                    flipped = jnp.where(diagonal[d], moved, flipped)
                lane = (g % 2) * flat + half * width
                out_ref[g // 2, pl.ds(out_start, per_atom), pl.ds(lane, width)] = flipped
        return carry

    lax.fori_loop(0, atoms, one_atom, 0)


def pick_tiles(green_pair, pair_index):
    energy_count = green_pair[0].shape[0]
    pair_count = pair_index.shape[0]
    partner = (pair_index % ATOMS).reshape(ATOMS, -1)
    target = jnp.repeat(partner, ORB, axis=1)
    return pl.pallas_call(
        pick_kernel,
        out_shape=jax.ShapeDtypeStruct((energy_count, pair_count, 2 * ORB * ORB), jnp.float32),
        in_specs=[
            pl.BlockSpec(memory_space=pltpu.VMEM),
            pl.BlockSpec(memory_space=pltpu.VMEM),
            pl.BlockSpec(memory_space=pltpu.VMEM),
        ],
        out_specs=pl.BlockSpec(memory_space=pltpu.VMEM),
    )(target, green_pair[0], green_pair[1])


def body(
    blocks, inverse_guess, coupling, pair_index, phonon_shift, phonon_strength, momentum_table
):
    local_blocks = (blocks[:, 0, 0, 0], blocks[:, 0, 0, 1])
    local_guess = (inverse_guess[:, 0, 0, 0], inverse_guess[:, 0, 0, 1])
    coupling_block = (coupling[0, 0, 0], coupling[0, 0, 1])
    energy_count = blocks.shape[0]
    green_pair = sweep(local_blocks, local_guess, coupling_block)
    green_block = jnp.stack(green_pair, axis=1)
    picked = pick_tiles(green_pair, pair_index[0])[:, None, None]
    momenta = momentum_table.shape[0]
    energy_groups = lax.axis_size("energy")
    mixing = phonon_matrix(
        phonon_shift, phonon_strength, momentum_table, energy_count * energy_groups
    )
    by_pairs = lax.all_to_all(
        picked, ("energy", "momentum"), split_axis=3, concat_axis=1, tiled=True
    )
    pair_count = by_pairs.shape[3]
    arranged = by_pairs.reshape(energy_count, energy_groups, momenta, pair_count, by_pairs.shape[4])
    mixing_grid = mixing.reshape(
        momenta, momenta, energy_groups, energy_count, energy_groups, energy_count
    )
    summed = jnp.einsum("kjabcd,dcjpx->bakpx", mixing_grid, arranged, precision=HIGHEST)
    summed = summed.reshape(energy_count, energy_groups * momenta, 1, pair_count, by_pairs.shape[4])
    self_energy = lax.all_to_all(
        summed, ("energy", "momentum"), split_axis=1, concat_axis=3, tiled=True
    )
    return (green_block[:, None, None], self_energy)


def solution(mesh):
    return jax.shard_map(
        body,
        mesh=mesh,
        in_specs=(
            P("energy", "momentum", "space", None, None, None),
            P("energy", "momentum", "space", None, None, None),
            P("momentum", "space", None, None, None),
            P("space", None),
            P(),
            P(),
            P(),
        ),
        out_specs=(
            P("energy", "momentum", "space", None, None, None),
            P("energy", "momentum", "space", None, None),
        ),
        check_vma=False,
    )
```

```python
import jax
import jax.numpy as jnp
from jax import lax
from jax.sharding import PartitionSpec as P
from jax.experimental import pallas as pl
from jax.experimental.pallas import tpu as pltpu

ORB = 16
ATOMS = 16
NEWTON = 2


HIGHEST = lax.Precision.HIGHEST
FIRST_STEP_PRECISION = lax.Precision.HIGHEST


def from_behind(shard, axis, by):
    count = lax.axis_size(axis)
    pairs = [(i, i + by) for i in range(count) if 0 <= i + by < count]
    return lax.ppermute(shard, axis, pairs)


def complex_product(first_factor, second_factor, precision=HIGHEST):
    first_real, first_imag = first_factor
    second_real, second_imag = second_factor
    real_part = jnp.matmul(first_real, second_real, precision=precision) - jnp.matmul(
        first_imag, second_imag, precision=precision
    )
    imag_part = jnp.matmul(first_real, second_imag, precision=precision) + jnp.matmul(
        first_imag, second_real, precision=precision
    )
    return (real_part, imag_part)


def newton_product(first_factor, second_factor):
    return complex_product(first_factor, second_factor, HIGHEST)


def first_step_product(first_factor, second_factor):
    return complex_product(first_factor, second_factor, FIRST_STEP_PRECISION)


def part(pair, rows=slice(None), cols=slice(None)):
    return tuple(value[..., rows, cols] for value in pair)


def combine(first_weight, first, second):
    return tuple(first_weight * a - b for a, b in zip(first, second))


def add(first, second):
    return tuple(a + b for a, b in zip(first, second))


def sweep(blocks, guess, coupling_block):
    space_count = lax.axis_size("space")
    size = blocks[0].shape[-1]
    edge = coupling_block[0].shape[-1]
    lead = slice(0, edge)
    trail = slice(size - edge, size)
    adjoint = (jnp.swapaxes(coupling_block[0], -1, -2), -jnp.swapaxes(coupling_block[1], -1, -2))

    def schur_of(incoming):
        return complex_product(complex_product(adjoint, incoming), coupling_block)

    def lead_rows_minus(values, schur, rows):
        update = newton_product(schur, rows)
        return tuple(v.at[..., lead, :].add(-u) for v, u in zip(values, update))

    first = combine(2.0, guess, first_step_product(guess, first_step_product(blocks, guess)))
    left = part(guess, cols=lead)
    right = part(guess, rows=lead)

    applied_trail = newton_product(blocks, part(first, cols=trail))
    boundary = combine(
        2.0, part(first, trail, trail), newton_product(part(first, rows=trail), applied_trail)
    )
    applied_left = newton_product(blocks, left)

    for section in range(1, space_count - 1):
        incoming = from_behind(boundary, "space", 1)
        schur = schur_of(incoming)
        mixed = first_step_product(schur, right)
        mixed_trail = part(mixed, cols=trail)
        step_trail = add(part(first, cols=trail), newton_product(left, mixed_trail))
        step_rows = add(part(first, rows=trail), newton_product(part(left, rows=trail), mixed))
        system_trail = add(applied_trail, newton_product(applied_left, mixed_trail))
        system_trail = lead_rows_minus(system_trail, schur, part(step_trail, rows=lead))
        boundary = combine(
            2.0, part(step_trail, rows=trail), newton_product(step_rows, system_trail)
        )

    applied = newton_product(blocks, first)
    if space_count > 1:
        incoming = from_behind(boundary, "space", 1)
        schur = schur_of(incoming)
        mixed = first_step_product(schur, right)
        step = add(first, newton_product(left, mixed))
        system_step = add(applied, newton_product(applied_left, mixed))
        system_step = lead_rows_minus(system_step, schur, part(step, rows=lead))
    else:
        step = first
        system_step = applied
    return combine(2.0, step, newton_product(step, system_step))


def phonon_matrix(phonon_shift, phonon_strength, momentum_table, energies):
    momenta = momentum_table.shape[0]
    chosen = (
        momentum_table[:, :, None] == jnp.arange(momenta, dtype=jnp.int32)[None, None, :]
    ).astype(jnp.float32)
    momentum_mix = jnp.einsum("kqj,dwq->kjdw", chosen, phonon_strength, precision=HIGHEST)
    energy_rows = jnp.arange(energies, dtype=jnp.int32)
    energy_gap = energy_rows[None, :] - energy_rows[:, None]
    emission = (energy_gap[None, :, :] == -phonon_shift[:, None, None]).astype(jnp.float32)
    absorption = (energy_gap[None, :, :] == phonon_shift[:, None, None]).astype(jnp.float32)
    shift_table = jnp.stack([emission, absorption], axis=0)
    return jnp.einsum("kjdw,dwEF->kjEF", momentum_mix, shift_table, precision=HIGHEST)


def pick_kernel(partner_ref, real_ref, imag_ref, out_ref):
    energy_count, size, _ = real_ref.shape
    atoms = size // ORB
    per_atom = partner_ref.shape[0] // atoms
    width = per_atom * ORB
    sublanes = 8
    flat = ORB * ORB
    halves = ORB // sublanes

    pick_rows = lax.broadcasted_iota(jnp.int32, (size, width), 0)
    pick_cols = lax.broadcasted_iota(jnp.int32, (size, width), 1)
    row_atom = pick_rows // ORB
    same_orbital = pick_rows % ORB == pick_cols % ORB
    grid_rows = lax.broadcasted_iota(jnp.int32, (sublanes, width), 0)
    grid_cols = lax.broadcasted_iota(jnp.int32, (sublanes, width), 1) // ORB
    diagonal = [(grid_cols - grid_rows) % per_atom == d for d in range(per_atom)]
    lane_tile = lax.broadcasted_iota(jnp.int32, (1, width), 1) // ORB

    def one_atom(atom, carry):
        target = jnp.zeros((1, width), jnp.int32)
        for j in range(per_atom):
            target = jnp.where(lane_tile == j, partner_ref[atom * per_atom + j], target)
        pick = jnp.where((row_atom == target) & same_orbital, 1.0, 0.0)
        start = pl.multiple_of(atom * ORB, ORB)
        stripes = []
        for e in range(energy_count):
            stripes.append(real_ref[e, pl.ds(start, ORB), :])
            stripes.append(imag_ref[e, pl.ds(start, ORB), :])
        stripes = jnp.concatenate(stripes, axis=0)
        chosen = jnp.dot(stripes, pick, precision=HIGHEST, preferred_element_type=jnp.float32)
        out_start = pl.multiple_of(atom * per_atom, per_atom)
        for g in range(2 * energy_count):
            for half in range(halves):
                row = g * ORB + half * sublanes
                grid = chosen[row : row + sublanes, :]
                flipped = grid
                for d in range(1, per_atom):
                    moved = pltpu.roll(grid, (sublanes - d) % sublanes, 0)
                    moved = pltpu.roll(moved, d * ORB, 1)
                    flipped = jnp.where(diagonal[d], moved, flipped)
                lane = (g % 2) * flat + half * width
                out_ref[g // 2, pl.ds(out_start, per_atom), pl.ds(lane, width)] = flipped
        return carry

    lax.fori_loop(0, atoms, one_atom, 0)


def pick_tiles(green_pair, pair_index):
    energy_count = green_pair[0].shape[0]
    pair_count = pair_index.shape[0]
    partner = pair_index % ATOMS
    return pl.pallas_call(
        pick_kernel,
        out_shape=jax.ShapeDtypeStruct((energy_count, pair_count, 2 * ORB * ORB), jnp.float32),
        in_specs=[
            pl.BlockSpec(memory_space=pltpu.SMEM),
            pl.BlockSpec(memory_space=pltpu.VMEM),
            pl.BlockSpec(memory_space=pltpu.VMEM),
        ],
        out_specs=pl.BlockSpec(memory_space=pltpu.VMEM),
    )(partner, green_pair[0], green_pair[1])


def body(
    blocks, inverse_guess, coupling, pair_index, phonon_shift, phonon_strength, momentum_table
):
    local_blocks = (blocks[:, 0, 0, 0], blocks[:, 0, 0, 1])
    local_guess = (inverse_guess[:, 0, 0, 0], inverse_guess[:, 0, 0, 1])
    coupling_block = (coupling[0, 0, 0], coupling[0, 0, 1])
    energy_count = blocks.shape[0]
    green_pair = sweep(local_blocks, local_guess, coupling_block)
    green_block = jnp.stack(green_pair, axis=1)
    picked = pick_tiles(green_pair, pair_index[0])[:, None, None]
    momenta = momentum_table.shape[0]
    energy_groups = lax.axis_size("energy")
    mixing = phonon_matrix(
        phonon_shift, phonon_strength, momentum_table, energy_count * energy_groups
    )
    by_pairs = lax.all_to_all(
        picked, ("energy", "momentum"), split_axis=3, concat_axis=1, tiled=True
    )
    pair_count = by_pairs.shape[3]
    arranged = by_pairs.reshape(energy_count, energy_groups, momenta, pair_count, by_pairs.shape[4])
    mixing_grid = mixing.reshape(
        momenta, momenta, energy_groups, energy_count, energy_groups, energy_count
    )
    summed = jnp.einsum("kjabcd,dcjpx->bakpx", mixing_grid, arranged, precision=HIGHEST)
    summed = summed.reshape(energy_count, energy_groups * momenta, 1, pair_count, by_pairs.shape[4])
    self_energy = lax.all_to_all(
        summed, ("energy", "momentum"), split_axis=1, concat_axis=3, tiled=True
    )
    return (green_block[:, None, None], self_energy)


def solution(mesh):
    return jax.shard_map(
        body,
        mesh=mesh,
        in_specs=(
            P("energy", "momentum", "space", None, None, None),
            P("energy", "momentum", "space", None, None, None),
            P("momentum", "space", None, None, None),
            P("space", None),
            P(),
            P(),
            P(),
        ),
        out_specs=(
            P("energy", "momentum", "space", None, None, None),
            P("energy", "momentum", "space", None, None),
        ),
        check_vma=False,
    )
```

```python
import jax
import jax.numpy as jnp
from jax import lax
from jax.sharding import PartitionSpec as P
from jax.experimental import pallas as pl
from jax.experimental.pallas import tpu as pltpu

ORB = 16
ATOMS = 16
NEWTON = 2


HIGHEST = lax.Precision.HIGHEST
FIRST_STEP_PRECISION = lax.Precision.HIGHEST


def from_behind(shard, axis, by):
    count = lax.axis_size(axis)
    pairs = [(i, i + by) for i in range(count) if 0 <= i + by < count]
    return lax.ppermute(shard, axis, pairs)


def complex_product(first_factor, second_factor, precision=HIGHEST):
    first_real, first_imag = first_factor
    second_real, second_imag = second_factor
    real_part = jnp.matmul(first_real, second_real, precision=precision) - jnp.matmul(
        first_imag, second_imag, precision=precision
    )
    imag_part = jnp.matmul(first_real, second_imag, precision=precision) + jnp.matmul(
        first_imag, second_real, precision=precision
    )
    return (real_part, imag_part)


def newton_product(first_factor, second_factor):
    return complex_product(first_factor, second_factor, HIGHEST)


def first_step_product(first_factor, second_factor):
    return complex_product(first_factor, second_factor, FIRST_STEP_PRECISION)


def part(pair, rows=slice(None), cols=slice(None)):
    return tuple(value[..., rows, cols] for value in pair)


def combine(first_weight, first, second):
    return tuple(first_weight * a - b for a, b in zip(first, second))


def add(first, second):
    return tuple(a + b for a, b in zip(first, second))


def sweep(blocks, guess, coupling_block):
    space_count = lax.axis_size("space")
    size = blocks[0].shape[-1]
    edge = coupling_block[0].shape[-1]
    lead = slice(0, edge)
    trail = slice(size - edge, size)
    adjoint = (jnp.swapaxes(coupling_block[0], -1, -2), -jnp.swapaxes(coupling_block[1], -1, -2))

    def schur_of(incoming):
        return complex_product(complex_product(adjoint, incoming), coupling_block)

    def lead_rows_minus(values, schur, rows):
        update = newton_product(schur, rows)
        return tuple(v.at[..., lead, :].add(-u) for v, u in zip(values, update))

    first = combine(2.0, guess, first_step_product(guess, first_step_product(blocks, guess)))
    left = part(guess, cols=lead)
    right = part(guess, rows=lead)

    applied_trail = newton_product(blocks, part(first, cols=trail))
    boundary = combine(
        2.0, part(first, trail, trail), newton_product(part(first, rows=trail), applied_trail)
    )
    applied_left = newton_product(blocks, left)

    for section in range(1, space_count - 1):
        incoming = from_behind(boundary, "space", 1)
        schur = schur_of(incoming)
        mixed = first_step_product(schur, right)
        mixed_trail = part(mixed, cols=trail)
        step_trail = add(part(first, cols=trail), newton_product(left, mixed_trail))
        step_rows = add(part(first, rows=trail), newton_product(part(left, rows=trail), mixed))
        system_trail = add(applied_trail, newton_product(applied_left, mixed_trail))
        system_trail = lead_rows_minus(system_trail, schur, part(step_trail, rows=lead))
        boundary = combine(
            2.0, part(step_trail, rows=trail), newton_product(step_rows, system_trail)
        )

    applied = newton_product(blocks, first)
    if space_count > 1:
        incoming = from_behind(boundary, "space", 1)
        schur = schur_of(incoming)
        mixed = first_step_product(schur, right)
        step = add(first, newton_product(left, mixed))
        system_step = add(applied, newton_product(applied_left, mixed))
        system_step = lead_rows_minus(system_step, schur, part(step, rows=lead))
    else:
        step = first
        system_step = applied
    return combine(2.0, step, newton_product(step, system_step))


def phonon_matrix(phonon_shift, phonon_strength, momentum_table, energies):
    momenta = momentum_table.shape[0]
    chosen = (
        momentum_table[:, :, None] == jnp.arange(momenta, dtype=jnp.int32)[None, None, :]
    ).astype(jnp.float32)
    momentum_mix = jnp.einsum("kqj,dwq->kjdw", chosen, phonon_strength, precision=HIGHEST)
    energy_rows = jnp.arange(energies, dtype=jnp.int32)
    energy_gap = energy_rows[None, :] - energy_rows[:, None]
    emission = (energy_gap[None, :, :] == -phonon_shift[:, None, None]).astype(jnp.float32)
    absorption = (energy_gap[None, :, :] == phonon_shift[:, None, None]).astype(jnp.float32)
    shift_table = jnp.stack([emission, absorption], axis=0)
    return jnp.einsum("kjdw,dwEF->kjEF", momentum_mix, shift_table, precision=HIGHEST)


def pick_kernel(partner_ref, real_ref, imag_ref, out_ref):
    energy_count, size, _ = real_ref.shape
    atoms = size // ORB
    per_atom = partner_ref.shape[0] // atoms
    width = per_atom * ORB
    sublanes = 8
    flat = ORB * ORB
    halves = ORB // sublanes

    pick_rows = lax.broadcasted_iota(jnp.int32, (size, width), 0)
    pick_cols = lax.broadcasted_iota(jnp.int32, (size, width), 1)
    row_atom = pick_rows // ORB
    same_orbital = pick_rows % ORB == pick_cols % ORB
    grid_rows = lax.broadcasted_iota(jnp.int32, (sublanes, width), 0)
    grid_cols = lax.broadcasted_iota(jnp.int32, (sublanes, width), 1) // ORB
    diagonal = [(grid_cols - grid_rows) % per_atom == d for d in range(per_atom)]
    lane_tile = lax.broadcasted_iota(jnp.int32, (1, width), 1) // ORB

    def one_atom(atom, carry):
        target = jnp.zeros((1, width), jnp.int32)
        for j in range(per_atom):
            target = jnp.where(lane_tile == j, partner_ref[atom * per_atom + j], target)
        pick = jnp.where((row_atom == target) & same_orbital, 1.0, 0.0)
        start = pl.multiple_of(atom * ORB, ORB)
        stripes = []
        for e in range(energy_count):
            stripes.append(real_ref[e, pl.ds(start, ORB), :])
            stripes.append(imag_ref[e, pl.ds(start, ORB), :])
        stripes = jnp.concatenate(stripes, axis=0)
        chosen = jnp.dot(stripes, pick, precision=HIGHEST, preferred_element_type=jnp.float32)
        out_start = pl.multiple_of(atom * per_atom, per_atom)
        for g in range(2 * energy_count):
            for half in range(halves):
                row = g * ORB + half * sublanes
                grid = chosen[row : row + sublanes, :]
                flipped = grid
                for d in range(1, per_atom):
                    moved = pltpu.roll(grid, (sublanes - d) % sublanes, 0)
                    moved = pltpu.roll(moved, d * ORB, 1)
                    flipped = jnp.where(diagonal[d], moved, flipped)
                lane = (g % 2) * flat + half * width
                out_ref[g // 2, pl.ds(out_start, per_atom), pl.ds(lane, width)] = flipped
        return carry

    lax.fori_loop(0, atoms, one_atom, 0)


def pick_tiles(green_pair, pair_index):
    energy_count = green_pair[0].shape[0]
    pair_count = pair_index.shape[0]
    partner = pair_index % ATOMS
    return pl.pallas_call(
        pick_kernel,
        out_shape=jax.ShapeDtypeStruct((energy_count, pair_count, 2 * ORB * ORB), jnp.float32),
        in_specs=[
            pl.BlockSpec(memory_space=pltpu.SMEM),
            pl.BlockSpec(memory_space=pltpu.VMEM),
            pl.BlockSpec(memory_space=pltpu.VMEM),
        ],
        out_specs=pl.BlockSpec(memory_space=pltpu.VMEM),
    )(partner, green_pair[0], green_pair[1])


def body(
    blocks, inverse_guess, coupling, pair_index, phonon_shift, phonon_strength, momentum_table
):
    coupling_block = (coupling[0, 0, 0], coupling[0, 0, 1])
    energy_count = blocks.shape[0]
    momenta = momentum_table.shape[0]
    energy_groups = lax.axis_size("energy")
    group = energy_groups * lax.axis_size("momentum")
    pair_count = pair_index.shape[1]
    width = 2 * ORB * ORB
    axes = ("energy", "momentum")
    green_parts = []
    received = []
    picked = None
    for e in range(energy_count):
        local_blocks = (blocks[e : e + 1, 0, 0, 0], blocks[e : e + 1, 0, 0, 1])
        local_guess = (inverse_guess[e : e + 1, 0, 0, 0], inverse_guess[e : e + 1, 0, 0, 1])
        if picked is not None:
            after = 0.0 * picked[0, 0]
            local_blocks = tuple(value + after for value in local_blocks)
        green_pair = sweep(local_blocks, local_guess, coupling_block)
        green_parts.append(jnp.stack(green_pair, axis=1))
        picked = pick_tiles(green_pair, pair_index[0])[0]
        received.append(lax.all_to_all(picked, axes, 0, 0, tiled=True))
    green_block = jnp.concatenate(green_parts, axis=0)
    mixing = phonon_matrix(
        phonon_shift, phonon_strength, momentum_table, energy_count * energy_groups
    )
    arranged = jnp.stack(received, axis=0).reshape(
        energy_count, energy_groups, momenta, pair_count // group, width
    )
    mixing_grid = mixing.reshape(
        momenta, momenta, energy_groups, energy_count, energy_groups, energy_count
    )
    summed = jnp.einsum("kjabcd,dcjpx->bakpx", mixing_grid, arranged, precision=HIGHEST)
    returned = [
        lax.all_to_all(summed[b].reshape(pair_count, width), axes, 0, 0, tiled=True)
        for b in range(energy_count)
    ]
    self_energy = jnp.stack(returned, axis=0)[:, None, None]
    return (green_block[:, None, None], self_energy)


def solution(mesh):
    return jax.shard_map(
        body,
        mesh=mesh,
        in_specs=(
            P("energy", "momentum", "space", None, None, None),
            P("energy", "momentum", "space", None, None, None),
            P("momentum", "space", None, None, None),
            P("space", None),
            P(),
            P(),
            P(),
        ),
        out_specs=(
            P("energy", "momentum", "space", None, None, None),
            P("energy", "momentum", "space", None, None),
        ),
        check_vma=False,
    )
```

```python
import jax
import jax.numpy as jnp
from jax import lax
from jax.sharding import PartitionSpec as P
from jax.experimental import pallas as pl
from jax.experimental.pallas import tpu as pltpu

ORB = 16
ATOMS = 16
NEWTON = 2


HIGHEST = lax.Precision.HIGHEST
FIRST_STEP_PRECISION = lax.Precision.HIGHEST


def from_behind(shard, axis, by):
    count = lax.axis_size(axis)
    pairs = [(i, i + by) for i in range(count) if 0 <= i + by < count]
    return lax.ppermute(shard, axis, pairs)


def complex_product(first_factor, second_factor, precision=HIGHEST):
    first_real, first_imag = first_factor
    second_real, second_imag = second_factor
    real_part = jnp.matmul(first_real, second_real, precision=precision) - jnp.matmul(
        first_imag, second_imag, precision=precision
    )
    imag_part = jnp.matmul(first_real, second_imag, precision=precision) + jnp.matmul(
        first_imag, second_real, precision=precision
    )
    return (real_part, imag_part)


def newton_product(first_factor, second_factor):
    return complex_product(first_factor, second_factor, HIGHEST)


def first_step_product(first_factor, second_factor):
    return complex_product(first_factor, second_factor, FIRST_STEP_PRECISION)


def part(pair, rows=slice(None), cols=slice(None)):
    return tuple(value[..., rows, cols] for value in pair)


def combine(first_weight, first, second):
    return tuple(first_weight * a - b for a, b in zip(first, second))


def add(first, second):
    return tuple(a + b for a, b in zip(first, second))


def sweep(blocks, guess, coupling_block):
    space_count = lax.axis_size("space")
    size = blocks[0].shape[-1]
    edge = coupling_block[0].shape[-1]
    lead = slice(0, edge)
    trail = slice(size - edge, size)
    adjoint = (jnp.swapaxes(coupling_block[0], -1, -2), -jnp.swapaxes(coupling_block[1], -1, -2))

    def schur_of(incoming):
        return complex_product(complex_product(adjoint, incoming), coupling_block)

    def lead_rows_minus(values, schur, rows):
        update = newton_product(schur, rows)
        return tuple(v.at[..., lead, :].add(-u) for v, u in zip(values, update))

    first = combine(2.0, guess, first_step_product(guess, first_step_product(blocks, guess)))
    left = part(guess, cols=lead)
    right = part(guess, rows=lead)

    applied_trail = newton_product(blocks, part(first, cols=trail))
    boundary = combine(
        2.0, part(first, trail, trail), newton_product(part(first, rows=trail), applied_trail)
    )
    applied_left = newton_product(blocks, left)

    for section in range(1, space_count - 1):
        incoming = from_behind(boundary, "space", 1)
        schur = schur_of(incoming)
        mixed = first_step_product(schur, right)
        mixed_trail = part(mixed, cols=trail)
        step_trail = add(part(first, cols=trail), newton_product(left, mixed_trail))
        step_rows = add(part(first, rows=trail), newton_product(part(left, rows=trail), mixed))
        system_trail = add(applied_trail, newton_product(applied_left, mixed_trail))
        system_trail = lead_rows_minus(system_trail, schur, part(step_trail, rows=lead))
        boundary = combine(
            2.0, part(step_trail, rows=trail), newton_product(step_rows, system_trail)
        )

    applied = newton_product(blocks, first)
    if space_count > 1:
        incoming = from_behind(boundary, "space", 1)
        schur = schur_of(incoming)
        mixed = first_step_product(schur, right)
        step = add(first, newton_product(left, mixed))
        system_step = add(applied, newton_product(applied_left, mixed))
        system_step = lead_rows_minus(system_step, schur, part(step, rows=lead))
    else:
        step = first
        system_step = applied
    return combine(2.0, step, newton_product(step, system_step))


def phonon_matrix(phonon_shift, phonon_strength, momentum_table, energies):
    momenta = momentum_table.shape[0]
    chosen = (
        momentum_table[:, :, None] == jnp.arange(momenta, dtype=jnp.int32)[None, None, :]
    ).astype(jnp.float32)
    momentum_mix = jnp.einsum("kqj,dwq->kjdw", chosen, phonon_strength, precision=HIGHEST)
    energy_rows = jnp.arange(energies, dtype=jnp.int32)
    energy_gap = energy_rows[None, :] - energy_rows[:, None]
    emission = (energy_gap[None, :, :] == -phonon_shift[:, None, None]).astype(jnp.float32)
    absorption = (energy_gap[None, :, :] == phonon_shift[:, None, None]).astype(jnp.float32)
    shift_table = jnp.stack([emission, absorption], axis=0)
    return jnp.einsum("kjdw,dwEF->kjEF", momentum_mix, shift_table, precision=HIGHEST)


def pick_kernel(partner_ref, real_ref, imag_ref, out_ref):
    energy_count, size, _ = real_ref.shape
    atoms = size // ORB
    per_atom = partner_ref.shape[0] // atoms
    width = per_atom * ORB
    sublanes = 8
    flat = ORB * ORB
    halves = ORB // sublanes

    pick_rows = lax.broadcasted_iota(jnp.int32, (size, width), 0)
    pick_cols = lax.broadcasted_iota(jnp.int32, (size, width), 1)
    row_atom = pick_rows // ORB
    same_orbital = pick_rows % ORB == pick_cols % ORB
    grid_rows = lax.broadcasted_iota(jnp.int32, (sublanes, width), 0)
    grid_cols = lax.broadcasted_iota(jnp.int32, (sublanes, width), 1) // ORB
    diagonal = [(grid_cols - grid_rows) % per_atom == d for d in range(per_atom)]
    lane_tile = lax.broadcasted_iota(jnp.int32, (1, width), 1) // ORB

    def one_atom(atom, carry):
        target = jnp.zeros((1, width), jnp.int32)
        for j in range(per_atom):
            target = jnp.where(lane_tile == j, partner_ref[atom * per_atom + j], target)
        pick = jnp.where((row_atom == target) & same_orbital, 1.0, 0.0)
        start = pl.multiple_of(atom * ORB, ORB)
        stripes = []
        for e in range(energy_count):
            stripes.append(real_ref[e, pl.ds(start, ORB), :])
            stripes.append(imag_ref[e, pl.ds(start, ORB), :])
        stripes = jnp.concatenate(stripes, axis=0)
        chosen = jnp.dot(stripes, pick, precision=HIGHEST, preferred_element_type=jnp.float32)
        out_start = pl.multiple_of(atom * per_atom, per_atom)
        for g in range(2 * energy_count):
            for half in range(halves):
                row = g * ORB + half * sublanes
                grid = chosen[row : row + sublanes, :]
                flipped = grid
                for d in range(1, per_atom):
                    moved = pltpu.roll(grid, (sublanes - d) % sublanes, 0)
                    moved = pltpu.roll(moved, d * ORB, 1)
                    flipped = jnp.where(diagonal[d], moved, flipped)
                lane = (g % 2) * flat + half * width
                out_ref[g // 2, pl.ds(out_start, per_atom), pl.ds(lane, width)] = flipped
        return carry

    lax.fori_loop(0, atoms, one_atom, 0)


def pick_tiles(green_pair, pair_index):
    energy_count = green_pair[0].shape[0]
    pair_count = pair_index.shape[0]
    partner = pair_index % ATOMS
    return pl.pallas_call(
        pick_kernel,
        out_shape=jax.ShapeDtypeStruct((energy_count, pair_count, 2 * ORB * ORB), jnp.float32),
        in_specs=[
            pl.BlockSpec(memory_space=pltpu.SMEM),
            pl.BlockSpec(memory_space=pltpu.VMEM),
            pl.BlockSpec(memory_space=pltpu.VMEM),
        ],
        out_specs=pl.BlockSpec(memory_space=pltpu.VMEM),
    )(partner, green_pair[0], green_pair[1])


def body(
    blocks, inverse_guess, coupling, pair_index, phonon_shift, phonon_strength, momentum_table
):
    local_blocks = (blocks[:, 0, 0, 0], blocks[:, 0, 0, 1])
    local_guess = (inverse_guess[:, 0, 0, 0], inverse_guess[:, 0, 0, 1])
    coupling_block = (coupling[0, 0, 0], coupling[0, 0, 1])
    energy_count = blocks.shape[0]
    green_pair = sweep(local_blocks, local_guess, coupling_block)
    green_block = jnp.stack(green_pair, axis=1)
    picked = pick_tiles(green_pair, pair_index[0])
    energy_groups = lax.axis_size("energy")
    mixing = phonon_matrix(
        phonon_shift, phonon_strength, momentum_table, energy_count * energy_groups
    )
    gathered = lax.all_gather(picked, "momentum", axis=0)
    momentum = lax.axis_index("momentum")
    own_energies = lax.axis_index("energy") * energy_count
    own_mixing = lax.dynamic_slice_in_dim(mixing[momentum], own_energies, energy_count, axis=2)
    partial = jnp.einsum("jEd,jdpx->Epx", own_mixing, gathered, precision=HIGHEST)
    self_energy = lax.psum_scatter(partial, "energy", scatter_dimension=0, tiled=True)
    self_energy = self_energy[:, None, None]
    return (green_block[:, None, None], self_energy)


def solution(mesh):
    return jax.shard_map(
        body,
        mesh=mesh,
        in_specs=(
            P("energy", "momentum", "space", None, None, None),
            P("energy", "momentum", "space", None, None, None),
            P("momentum", "space", None, None, None),
            P("space", None),
            P(),
            P(),
            P(),
        ),
        out_specs=(
            P("energy", "momentum", "space", None, None, None),
            P("energy", "momentum", "space", None, None),
        ),
        check_vma=False,
    )
```

```python
import jax
import jax.numpy as jnp
from jax import lax
from jax.sharding import PartitionSpec as P
from jax.experimental import pallas as pl
from jax.experimental.pallas import tpu as pltpu

ORB = 16
ATOMS = 16
NEWTON = 2


HIGHEST = lax.Precision.HIGHEST
FIRST_STEP_PRECISION = lax.Precision.HIGHEST


def from_behind(shard, axis, by):
    count = lax.axis_size(axis)
    pairs = [(i, i + by) for i in range(count) if 0 <= i + by < count]
    return lax.ppermute(shard, axis, pairs)


def complex_product(first_factor, second_factor, precision=HIGHEST):
    first_real, first_imag = first_factor
    second_real, second_imag = second_factor
    real_real = jnp.matmul(first_real, second_real, precision=precision)
    imag_imag = jnp.matmul(first_imag, second_imag, precision=precision)
    summed = jnp.matmul(
        first_real + first_imag, second_real + second_imag, precision=precision
    )
    return (real_real - imag_imag, summed - real_real - imag_imag)


def newton_product(first_factor, second_factor):
    return complex_product(first_factor, second_factor, HIGHEST)


def first_step_product(first_factor, second_factor):
    return complex_product(first_factor, second_factor, FIRST_STEP_PRECISION)


def part(pair, rows=slice(None), cols=slice(None)):
    return tuple(value[..., rows, cols] for value in pair)


def combine(first_weight, first, second):
    return tuple(first_weight * a - b for a, b in zip(first, second))


def add(first, second):
    return tuple(a + b for a, b in zip(first, second))


def sweep(blocks, guess, coupling_block):
    space_count = lax.axis_size("space")
    size = blocks[0].shape[-1]
    edge = coupling_block[0].shape[-1]
    lead = slice(0, edge)
    trail = slice(size - edge, size)
    adjoint = (jnp.swapaxes(coupling_block[0], -1, -2), -jnp.swapaxes(coupling_block[1], -1, -2))

    def schur_of(incoming):
        return complex_product(complex_product(adjoint, incoming), coupling_block)

    def lead_rows_minus(values, schur, rows):
        update = newton_product(schur, rows)
        return tuple(v.at[..., lead, :].add(-u) for v, u in zip(values, update))

    first = combine(2.0, guess, first_step_product(guess, first_step_product(blocks, guess)))
    left = part(guess, cols=lead)
    right = part(guess, rows=lead)

    applied_trail = newton_product(blocks, part(first, cols=trail))
    boundary = combine(
        2.0, part(first, trail, trail), newton_product(part(first, rows=trail), applied_trail)
    )
    applied_left = newton_product(blocks, left)

    for section in range(1, space_count - 1):
        incoming = from_behind(boundary, "space", 1)
        schur = schur_of(incoming)
        mixed = first_step_product(schur, right)
        mixed_trail = part(mixed, cols=trail)
        step_trail = add(part(first, cols=trail), newton_product(left, mixed_trail))
        step_rows = add(part(first, rows=trail), newton_product(part(left, rows=trail), mixed))
        system_trail = add(applied_trail, newton_product(applied_left, mixed_trail))
        system_trail = lead_rows_minus(system_trail, schur, part(step_trail, rows=lead))
        boundary = combine(
            2.0, part(step_trail, rows=trail), newton_product(step_rows, system_trail)
        )

    applied = newton_product(blocks, first)
    if space_count > 1:
        incoming = from_behind(boundary, "space", 1)
        schur = schur_of(incoming)
        mixed = first_step_product(schur, right)
        step = add(first, newton_product(left, mixed))
        system_step = add(applied, newton_product(applied_left, mixed))
        system_step = lead_rows_minus(system_step, schur, part(step, rows=lead))
    else:
        step = first
        system_step = applied
    return combine(2.0, step, newton_product(step, system_step))


def phonon_matrix(phonon_shift, phonon_strength, momentum_table, energies):
    momenta = momentum_table.shape[0]
    chosen = (
        momentum_table[:, :, None] == jnp.arange(momenta, dtype=jnp.int32)[None, None, :]
    ).astype(jnp.float32)
    momentum_mix = jnp.einsum("kqj,dwq->kjdw", chosen, phonon_strength, precision=HIGHEST)
    energy_rows = jnp.arange(energies, dtype=jnp.int32)
    energy_gap = energy_rows[None, :] - energy_rows[:, None]
    emission = (energy_gap[None, :, :] == -phonon_shift[:, None, None]).astype(jnp.float32)
    absorption = (energy_gap[None, :, :] == phonon_shift[:, None, None]).astype(jnp.float32)
    shift_table = jnp.stack([emission, absorption], axis=0)
    return jnp.einsum("kjdw,dwEF->kjEF", momentum_mix, shift_table, precision=HIGHEST)


def pick_kernel(partner_ref, real_ref, imag_ref, out_ref):
    energy_count, size, _ = real_ref.shape
    atoms = size // ORB
    per_atom = partner_ref.shape[0] // atoms
    width = per_atom * ORB
    sublanes = 8
    flat = ORB * ORB
    halves = ORB // sublanes

    pick_rows = lax.broadcasted_iota(jnp.int32, (size, width), 0)
    pick_cols = lax.broadcasted_iota(jnp.int32, (size, width), 1)
    row_atom = pick_rows // ORB
    same_orbital = pick_rows % ORB == pick_cols % ORB
    grid_rows = lax.broadcasted_iota(jnp.int32, (sublanes, width), 0)
    grid_cols = lax.broadcasted_iota(jnp.int32, (sublanes, width), 1) // ORB
    diagonal = [(grid_cols - grid_rows) % per_atom == d for d in range(per_atom)]
    lane_tile = lax.broadcasted_iota(jnp.int32, (1, width), 1) // ORB

    def one_atom(atom, carry):
        target = jnp.zeros((1, width), jnp.int32)
        for j in range(per_atom):
            target = jnp.where(lane_tile == j, partner_ref[atom * per_atom + j], target)
        pick = jnp.where((row_atom == target) & same_orbital, 1.0, 0.0)
        start = pl.multiple_of(atom * ORB, ORB)
        stripes = []
        for e in range(energy_count):
            stripes.append(real_ref[e, pl.ds(start, ORB), :])
            stripes.append(imag_ref[e, pl.ds(start, ORB), :])
        stripes = jnp.concatenate(stripes, axis=0)
        chosen = jnp.dot(stripes, pick, precision=HIGHEST, preferred_element_type=jnp.float32)
        out_start = pl.multiple_of(atom * per_atom, per_atom)
        for g in range(2 * energy_count):
            for half in range(halves):
                row = g * ORB + half * sublanes
                grid = chosen[row : row + sublanes, :]
                flipped = grid
                for d in range(1, per_atom):
                    moved = pltpu.roll(grid, (sublanes - d) % sublanes, 0)
                    moved = pltpu.roll(moved, d * ORB, 1)
                    flipped = jnp.where(diagonal[d], moved, flipped)
                lane = (g % 2) * flat + half * width
                out_ref[g // 2, pl.ds(out_start, per_atom), pl.ds(lane, width)] = flipped
        return carry

    lax.fori_loop(0, atoms, one_atom, 0)


def pick_tiles(green_pair, pair_index):
    energy_count = green_pair[0].shape[0]
    pair_count = pair_index.shape[0]
    partner = pair_index % ATOMS
    return pl.pallas_call(
        pick_kernel,
        out_shape=jax.ShapeDtypeStruct((energy_count, pair_count, 2 * ORB * ORB), jnp.float32),
        in_specs=[
            pl.BlockSpec(memory_space=pltpu.SMEM),
            pl.BlockSpec(memory_space=pltpu.VMEM),
            pl.BlockSpec(memory_space=pltpu.VMEM),
        ],
        out_specs=pl.BlockSpec(memory_space=pltpu.VMEM),
    )(partner, green_pair[0], green_pair[1])


def body(
    blocks, inverse_guess, coupling, pair_index, phonon_shift, phonon_strength, momentum_table
):
    local_blocks = (blocks[:, 0, 0, 0], blocks[:, 0, 0, 1])
    local_guess = (inverse_guess[:, 0, 0, 0], inverse_guess[:, 0, 0, 1])
    coupling_block = (coupling[0, 0, 0], coupling[0, 0, 1])
    energy_count = blocks.shape[0]
    green_pair = sweep(local_blocks, local_guess, coupling_block)
    green_block = jnp.stack(green_pair, axis=1)
    picked = pick_tiles(green_pair, pair_index[0])[:, None, None]
    momenta = momentum_table.shape[0]
    energy_groups = lax.axis_size("energy")
    mixing = phonon_matrix(
        phonon_shift, phonon_strength, momentum_table, energy_count * energy_groups
    )
    by_pairs = lax.all_to_all(
        picked, ("energy", "momentum"), split_axis=3, concat_axis=1, tiled=True
    )
    pair_count = by_pairs.shape[3]
    arranged = by_pairs.reshape(energy_count, energy_groups, momenta, pair_count, by_pairs.shape[4])
    mixing_grid = mixing.reshape(
        momenta, momenta, energy_groups, energy_count, energy_groups, energy_count
    )
    summed = jnp.einsum("kjabcd,dcjpx->bakpx", mixing_grid, arranged, precision=HIGHEST)
    summed = summed.reshape(energy_count, energy_groups * momenta, 1, pair_count, by_pairs.shape[4])
    self_energy = lax.all_to_all(
        summed, ("energy", "momentum"), split_axis=1, concat_axis=3, tiled=True
    )
    return (green_block[:, None, None], self_energy)


def solution(mesh):
    return jax.shard_map(
        body,
        mesh=mesh,
        in_specs=(
            P("energy", "momentum", "space", None, None, None),
            P("energy", "momentum", "space", None, None, None),
            P("momentum", "space", None, None, None),
            P("space", None),
            P(),
            P(),
            P(),
        ),
        out_specs=(
            P("energy", "momentum", "space", None, None, None),
            P("energy", "momentum", "space", None, None),
        ),
        check_vma=False,
    )
```

```python
import jax
import jax.numpy as jnp
from jax import lax
from jax.sharding import PartitionSpec as P
from jax.experimental import pallas as pl
from jax.experimental.pallas import tpu as pltpu

ORB = 16
ATOMS = 16
NEWTON = 2


HIGHEST = lax.Precision.HIGHEST
FIRST_STEP_PRECISION = lax.Precision.HIGHEST


def from_behind(shard, axis, by):
    count = lax.axis_size(axis)
    pairs = [(i, i + by) for i in range(count) if 0 <= i + by < count]
    return lax.ppermute(shard, axis, pairs)


def complex_product(first_factor, second_factor, precision=HIGHEST):
    first_real, first_imag = first_factor
    second_real, second_imag = second_factor
    real_real = jnp.matmul(first_real, second_real, precision=precision)
    imag_imag = jnp.matmul(first_imag, second_imag, precision=precision)
    summed = jnp.matmul(
        first_real + first_imag, second_real + second_imag, precision=precision
    )
    return (real_real - imag_imag, summed - real_real - imag_imag)


def newton_product(first_factor, second_factor):
    return complex_product(first_factor, second_factor, HIGHEST)


def first_step_product(first_factor, second_factor):
    return complex_product(first_factor, second_factor, FIRST_STEP_PRECISION)


def part(pair, rows=slice(None), cols=slice(None)):
    return tuple(value[..., rows, cols] for value in pair)


def combine(first_weight, first, second):
    return tuple(first_weight * a - b for a, b in zip(first, second))


def add(first, second):
    return tuple(a + b for a, b in zip(first, second))


def sweep(blocks, guess, coupling_block):
    space_count = lax.axis_size("space")
    size = blocks[0].shape[-1]
    edge = coupling_block[0].shape[-1]
    lead = slice(0, edge)
    trail = slice(size - edge, size)
    adjoint = (jnp.swapaxes(coupling_block[0], -1, -2), -jnp.swapaxes(coupling_block[1], -1, -2))

    def schur_of(incoming):
        return complex_product(complex_product(adjoint, incoming), coupling_block)

    def lead_rows_minus(values, schur, rows):
        update = newton_product(schur, rows)
        return tuple(v.at[..., lead, :].add(-u) for v, u in zip(values, update))

    first = combine(2.0, guess, first_step_product(guess, first_step_product(blocks, guess)))
    left = part(guess, cols=lead)
    right = part(guess, rows=lead)

    applied_trail = newton_product(blocks, part(first, cols=trail))
    boundary = combine(
        2.0, part(first, trail, trail), newton_product(part(first, rows=trail), applied_trail)
    )
    applied_left = newton_product(blocks, left)

    for section in range(1, space_count - 1):
        incoming = from_behind(boundary, "space", 1)
        schur = schur_of(incoming)
        mixed = first_step_product(schur, right)
        mixed_trail = part(mixed, cols=trail)
        step_trail = add(part(first, cols=trail), newton_product(left, mixed_trail))
        step_rows = add(part(first, rows=trail), newton_product(part(left, rows=trail), mixed))
        system_trail = add(applied_trail, newton_product(applied_left, mixed_trail))
        system_trail = lead_rows_minus(system_trail, schur, part(step_trail, rows=lead))
        boundary = combine(
            2.0, part(step_trail, rows=trail), newton_product(step_rows, system_trail)
        )

    applied = newton_product(blocks, first)
    if space_count > 1:
        incoming = from_behind(boundary, "space", 1)
        schur = schur_of(incoming)
        mixed = first_step_product(schur, right)
        step = add(first, newton_product(left, mixed))
        system_step = add(applied, newton_product(applied_left, mixed))
        system_step = lead_rows_minus(system_step, schur, part(step, rows=lead))
    else:
        step = first
        system_step = applied
    return combine(2.0, step, newton_product(step, system_step))


def phonon_matrix(phonon_shift, phonon_strength, momentum_table, energies):
    momenta = momentum_table.shape[0]
    chosen = (
        momentum_table[:, :, None] == jnp.arange(momenta, dtype=jnp.int32)[None, None, :]
    ).astype(jnp.float32)
    momentum_mix = jnp.einsum("kqj,dwq->kjdw", chosen, phonon_strength, precision=HIGHEST)
    energy_rows = jnp.arange(energies, dtype=jnp.int32)
    energy_gap = energy_rows[None, :] - energy_rows[:, None]
    emission = (energy_gap[None, :, :] == -phonon_shift[:, None, None]).astype(jnp.float32)
    absorption = (energy_gap[None, :, :] == phonon_shift[:, None, None]).astype(jnp.float32)
    shift_table = jnp.stack([emission, absorption], axis=0)
    return jnp.einsum("kjdw,dwEF->kjEF", momentum_mix, shift_table, precision=HIGHEST)


def pick_kernel(partner_ref, real_ref, imag_ref, out_ref):
    energy_count, size, _ = real_ref.shape
    atoms = size // ORB
    per_atom = partner_ref.shape[0] // atoms
    width = per_atom * ORB
    sublanes = 8
    flat = ORB * ORB
    halves = ORB // sublanes

    pick_rows = lax.broadcasted_iota(jnp.int32, (size, width), 0)
    pick_cols = lax.broadcasted_iota(jnp.int32, (size, width), 1)
    row_atom = pick_rows // ORB
    same_orbital = pick_rows % ORB == pick_cols % ORB
    grid_rows = lax.broadcasted_iota(jnp.int32, (sublanes, width), 0)
    grid_cols = lax.broadcasted_iota(jnp.int32, (sublanes, width), 1) // ORB
    diagonal = [(grid_cols - grid_rows) % per_atom == d for d in range(per_atom)]
    lane_tile = lax.broadcasted_iota(jnp.int32, (1, width), 1) // ORB

    def one_atom(atom, carry):
        target = jnp.zeros((1, width), jnp.int32)
        for j in range(per_atom):
            target = jnp.where(lane_tile == j, partner_ref[atom * per_atom + j], target)
        pick = jnp.where((row_atom == target) & same_orbital, 1.0, 0.0).astype(jnp.bfloat16)
        start = pl.multiple_of(atom * ORB, ORB)
        stripes = []
        for e in range(energy_count):
            stripes.append(real_ref[e, pl.ds(start, ORB), :])
            stripes.append(imag_ref[e, pl.ds(start, ORB), :])
        stripes = jnp.concatenate(stripes, axis=0)
        high = stripes.astype(jnp.bfloat16)
        rest = stripes - high.astype(jnp.float32)
        middle = rest.astype(jnp.bfloat16)
        low = (rest - middle.astype(jnp.float32)).astype(jnp.bfloat16)
        pieces = jnp.concatenate([high, middle, low], axis=0)
        selected = jnp.dot(pieces, pick, preferred_element_type=jnp.float32)
        rows = stripes.shape[0]
        chosen = (selected[:rows] + selected[rows : 2 * rows]) + selected[2 * rows :]
        out_start = pl.multiple_of(atom * per_atom, per_atom)
        for g in range(2 * energy_count):
            for half in range(halves):
                row = g * ORB + half * sublanes
                grid = chosen[row : row + sublanes, :]
                flipped = grid
                for d in range(1, per_atom):
                    moved = pltpu.roll(grid, (sublanes - d) % sublanes, 0)
                    moved = pltpu.roll(moved, d * ORB, 1)
                    flipped = jnp.where(diagonal[d], moved, flipped)
                lane = (g % 2) * flat + half * width
                out_ref[g // 2, pl.ds(out_start, per_atom), pl.ds(lane, width)] = flipped
        return carry

    lax.fori_loop(0, atoms, one_atom, 0)


def pick_tiles(green_pair, pair_index):
    energy_count = green_pair[0].shape[0]
    pair_count = pair_index.shape[0]
    partner = pair_index % ATOMS
    return pl.pallas_call(
        pick_kernel,
        out_shape=jax.ShapeDtypeStruct((energy_count, pair_count, 2 * ORB * ORB), jnp.float32),
        in_specs=[
            pl.BlockSpec(memory_space=pltpu.SMEM),
            pl.BlockSpec(memory_space=pltpu.VMEM),
            pl.BlockSpec(memory_space=pltpu.VMEM),
        ],
        out_specs=pl.BlockSpec(memory_space=pltpu.VMEM),
    )(partner, green_pair[0], green_pair[1])


def body(
    blocks, inverse_guess, coupling, pair_index, phonon_shift, phonon_strength, momentum_table
):
    local_blocks = (blocks[:, 0, 0, 0], blocks[:, 0, 0, 1])
    local_guess = (inverse_guess[:, 0, 0, 0], inverse_guess[:, 0, 0, 1])
    coupling_block = (coupling[0, 0, 0], coupling[0, 0, 1])
    energy_count = blocks.shape[0]
    green_pair = sweep(local_blocks, local_guess, coupling_block)
    green_block = jnp.stack(green_pair, axis=1)
    picked = pick_tiles(green_pair, pair_index[0])[:, None, None]
    momenta = momentum_table.shape[0]
    energy_groups = lax.axis_size("energy")
    mixing = phonon_matrix(
        phonon_shift, phonon_strength, momentum_table, energy_count * energy_groups
    )
    by_pairs = lax.all_to_all(
        picked, ("energy", "momentum"), split_axis=3, concat_axis=1, tiled=True
    )
    pair_count = by_pairs.shape[3]
    arranged = by_pairs.reshape(energy_count, energy_groups, momenta, pair_count, by_pairs.shape[4])
    mixing_grid = mixing.reshape(
        momenta, momenta, energy_groups, energy_count, energy_groups, energy_count
    )
    summed = jnp.einsum("kjabcd,dcjpx->bakpx", mixing_grid, arranged, precision=HIGHEST)
    summed = summed.reshape(energy_count, energy_groups * momenta, 1, pair_count, by_pairs.shape[4])
    self_energy = lax.all_to_all(
        summed, ("energy", "momentum"), split_axis=1, concat_axis=3, tiled=True
    )
    return (green_block[:, None, None], self_energy)


def solution(mesh):
    return jax.shard_map(
        body,
        mesh=mesh,
        in_specs=(
            P("energy", "momentum", "space", None, None, None),
            P("energy", "momentum", "space", None, None, None),
            P("momentum", "space", None, None, None),
            P("space", None),
            P(),
            P(),
            P(),
        ),
        out_specs=(
            P("energy", "momentum", "space", None, None, None),
            P("energy", "momentum", "space", None, None),
        ),
        check_vma=False,
    )
```

```python
import jax
import jax.numpy as jnp
from jax import lax
from jax.sharding import PartitionSpec as P
from jax.experimental import pallas as pl
from jax.experimental.pallas import tpu as pltpu

ORB = 16
ATOMS = 16
NEWTON = 2


HIGHEST = lax.Precision.HIGHEST
FIRST_STEP_PRECISION = lax.Precision.HIGHEST


def from_behind(shard, axis, by):
    count = lax.axis_size(axis)
    pairs = [(i, i + by) for i in range(count) if 0 <= i + by < count]
    return lax.ppermute(shard, axis, pairs)


def complex_product(first_factor, second_factor, precision=HIGHEST):
    first_real, first_imag = first_factor
    second_real, second_imag = second_factor
    real_real = jnp.matmul(first_real, second_real, precision=precision)
    imag_imag = jnp.matmul(first_imag, second_imag, precision=precision)
    summed = jnp.matmul(
        first_real + first_imag, second_real + second_imag, precision=precision
    )
    return (real_real - imag_imag, summed - real_real - imag_imag)


def newton_product(first_factor, second_factor):
    return complex_product(first_factor, second_factor, HIGHEST)


def first_step_product(first_factor, second_factor):
    return complex_product(first_factor, second_factor, FIRST_STEP_PRECISION)


def part(pair, rows=slice(None), cols=slice(None)):
    return tuple(value[..., rows, cols] for value in pair)


def combine(first_weight, first, second):
    return tuple(first_weight * a - b for a, b in zip(first, second))


def add(first, second):
    return tuple(a + b for a, b in zip(first, second))


def sweep(blocks, guess, coupling_block):
    space_count = lax.axis_size("space")
    size = blocks[0].shape[-1]
    edge = coupling_block[0].shape[-1]
    lead = slice(0, edge)
    trail = slice(size - edge, size)
    adjoint = (jnp.swapaxes(coupling_block[0], -1, -2), -jnp.swapaxes(coupling_block[1], -1, -2))

    def schur_of(incoming):
        return complex_product(complex_product(adjoint, incoming), coupling_block)

    def lead_rows_minus(values, schur, rows):
        update = newton_product(schur, rows)
        return tuple(v.at[..., lead, :].add(-u) for v, u in zip(values, update))

    first = combine(2.0, guess, first_step_product(guess, first_step_product(blocks, guess)))
    left = part(guess, cols=lead)
    right = part(guess, rows=lead)

    applied_trail = newton_product(blocks, part(first, cols=trail))
    boundary = combine(
        2.0, part(first, trail, trail), newton_product(part(first, rows=trail), applied_trail)
    )
    applied_left = newton_product(blocks, left)

    for section in range(1, space_count - 1):
        incoming = from_behind(boundary, "space", 1)
        schur = schur_of(incoming)
        mixed = first_step_product(schur, right)
        mixed_trail = part(mixed, cols=trail)
        step_trail = add(part(first, cols=trail), newton_product(left, mixed_trail))
        step_rows = add(part(first, rows=trail), newton_product(part(left, rows=trail), mixed))
        system_trail = add(applied_trail, newton_product(applied_left, mixed_trail))
        system_trail = lead_rows_minus(system_trail, schur, part(step_trail, rows=lead))
        boundary = combine(
            2.0, part(step_trail, rows=trail), newton_product(step_rows, system_trail)
        )

    applied = newton_product(blocks, first)
    if space_count > 1:
        incoming = from_behind(boundary, "space", 1)
        schur = schur_of(incoming)
        mixed = first_step_product(schur, right)
        step = add(first, newton_product(left, mixed))
        system_step = add(applied, newton_product(applied_left, mixed))
        system_step = lead_rows_minus(system_step, schur, part(step, rows=lead))
    else:
        step = first
        system_step = applied
    return combine(2.0, step, newton_product(step, system_step))


def phonon_matrix(phonon_shift, phonon_strength, momentum_table, energies):
    momenta = momentum_table.shape[0]
    chosen = (
        momentum_table[:, :, None] == jnp.arange(momenta, dtype=jnp.int32)[None, None, :]
    ).astype(jnp.float32)
    momentum_mix = jnp.einsum("kqj,dwq->kjdw", chosen, phonon_strength, precision=HIGHEST)
    energy_rows = jnp.arange(energies, dtype=jnp.int32)
    energy_gap = energy_rows[None, :] - energy_rows[:, None]
    emission = (energy_gap[None, :, :] == -phonon_shift[:, None, None]).astype(jnp.float32)
    absorption = (energy_gap[None, :, :] == phonon_shift[:, None, None]).astype(jnp.float32)
    shift_table = jnp.stack([emission, absorption], axis=0)
    return jnp.einsum("kjdw,dwEF->kjEF", momentum_mix, shift_table, precision=HIGHEST)


def pick_kernel(partner_ref, real_ref, imag_ref, out_ref):
    energy_count, size, _ = real_ref.shape
    chunk = out_ref.shape[2]
    atoms = size // ORB
    per_atom = partner_ref.shape[0] // atoms
    width = per_atom * ORB
    sublanes = 8
    flat = ORB * ORB
    halves = ORB // sublanes

    pick_rows = lax.broadcasted_iota(jnp.int32, (size, width), 0)
    pick_cols = lax.broadcasted_iota(jnp.int32, (size, width), 1)
    row_atom = pick_rows // ORB
    same_orbital = pick_rows % ORB == pick_cols % ORB
    grid_rows = lax.broadcasted_iota(jnp.int32, (sublanes, width), 0)
    grid_cols = lax.broadcasted_iota(jnp.int32, (sublanes, width), 1) // ORB
    diagonal = [(grid_cols - grid_rows) % per_atom == d for d in range(per_atom)]
    lane_tile = lax.broadcasted_iota(jnp.int32, (1, width), 1) // ORB

    def one_atom(atom, carry):
        target = jnp.zeros((1, width), jnp.int32)
        for j in range(per_atom):
            target = jnp.where(lane_tile == j, partner_ref[atom * per_atom + j], target)
        pick = jnp.where((row_atom == target) & same_orbital, 1.0, 0.0).astype(jnp.bfloat16)
        start = pl.multiple_of(atom * ORB, ORB)
        stripes = []
        for e in range(energy_count):
            stripes.append(real_ref[e, pl.ds(start, ORB), :])
            stripes.append(imag_ref[e, pl.ds(start, ORB), :])
        stripes = jnp.concatenate(stripes, axis=0)
        high = stripes.astype(jnp.bfloat16)
        rest = stripes - high.astype(jnp.float32)
        middle = rest.astype(jnp.bfloat16)
        low = (rest - middle.astype(jnp.float32)).astype(jnp.bfloat16)
        pieces = jnp.concatenate([high, middle, low], axis=0)
        selected = jnp.dot(pieces, pick, preferred_element_type=jnp.float32)
        rows = stripes.shape[0]
        chosen = (selected[:rows] + selected[rows : 2 * rows]) + selected[2 * rows :]
        out_start = pl.multiple_of(atom * per_atom, per_atom)
        for g in range(2 * energy_count):
            for half in range(halves):
                row = g * ORB + half * sublanes
                grid = chosen[row : row + sublanes, :]
                flipped = grid
                for d in range(1, per_atom):
                    moved = pltpu.roll(grid, (sublanes - d) % sublanes, 0)
                    moved = pltpu.roll(moved, d * ORB, 1)
                    flipped = jnp.where(diagonal[d], moved, flipped)
                lane = (g % 2) * flat + half * width
                if chunk >= per_atom:
                    out_ref[
                        out_start // chunk, g // 2, pl.ds(out_start % chunk, per_atom), pl.ds(lane, width)
                    ] = flipped
                else:
                    for q in range(per_atom // chunk):
                        out_ref[
                            atom * (per_atom // chunk) + q, g // 2, :, pl.ds(lane, width)
                        ] = flipped[q * chunk : (q + 1) * chunk]
        return carry

    lax.fori_loop(0, atoms, one_atom, 0)


def pick_tiles(green_pair, pair_index, chunks):
    energy_count = green_pair[0].shape[0]
    pair_count = pair_index.shape[0]
    partner = pair_index % ATOMS
    shape = (chunks, energy_count, pair_count // chunks, 2 * ORB * ORB)
    return pl.pallas_call(
        pick_kernel,
        out_shape=jax.ShapeDtypeStruct(shape, jnp.float32),
        in_specs=[
            pl.BlockSpec(memory_space=pltpu.SMEM),
            pl.BlockSpec(memory_space=pltpu.VMEM),
            pl.BlockSpec(memory_space=pltpu.VMEM),
        ],
        out_specs=pl.BlockSpec(memory_space=pltpu.VMEM),
    )(partner, green_pair[0], green_pair[1])


def body(
    blocks, inverse_guess, coupling, pair_index, phonon_shift, phonon_strength, momentum_table
):
    local_blocks = (blocks[:, 0, 0, 0], blocks[:, 0, 0, 1])
    local_guess = (inverse_guess[:, 0, 0, 0], inverse_guess[:, 0, 0, 1])
    coupling_block = (coupling[0, 0, 0], coupling[0, 0, 1])
    energy_count = blocks.shape[0]
    green_pair = sweep(local_blocks, local_guess, coupling_block)
    green_block = jnp.stack(green_pair, axis=1)
    momenta = momentum_table.shape[0]
    energy_groups = lax.axis_size("energy")
    axes = ("energy", "momentum")
    group = energy_groups * lax.axis_size("momentum")
    pair_count = pair_index.shape[1]
    width = 2 * ORB * ORB
    picked = pick_tiles(green_pair, pair_index[0], group)
    mixing = phonon_matrix(
        phonon_shift, phonon_strength, momentum_table, energy_count * energy_groups
    )
    by_pairs = lax.all_to_all(picked, axes, 0, 0, tiled=True)
    arranged = by_pairs.reshape(energy_groups, momenta, energy_count, pair_count // group, width)
    mixing_grid = mixing.reshape(
        momenta, momenta, energy_groups, energy_count, energy_groups, energy_count
    )
    summed = jnp.einsum("kjabcd,cjdpx->akbpx", mixing_grid, arranged, precision=HIGHEST)
    summed = summed.reshape(group, energy_count, pair_count // group, width)
    self_energy = lax.all_to_all(summed, axes, 0, 2, tiled=True)
    self_energy = self_energy.reshape(energy_count, 1, 1, pair_count, width)
    return (green_block[:, None, None], self_energy)


def solution(mesh):
    return jax.shard_map(
        body,
        mesh=mesh,
        in_specs=(
            P("energy", "momentum", "space", None, None, None),
            P("energy", "momentum", "space", None, None, None),
            P("momentum", "space", None, None, None),
            P("space", None),
            P(),
            P(),
            P(),
        ),
        out_specs=(
            P("energy", "momentum", "space", None, None, None),
            P("energy", "momentum", "space", None, None),
        ),
        check_vma=False,
    )
```

```python
import jax
import jax.numpy as jnp
from jax import lax
from jax.sharding import PartitionSpec as P
from jax.experimental import pallas as pl
from jax.experimental.pallas import tpu as pltpu

ORB = 16
ATOMS = 16
NEWTON = 2


HIGHEST = lax.Precision.HIGHEST
FIRST_STEP_PRECISION = lax.Precision.HIGHEST


def from_behind(shard, axis, by):
    count = lax.axis_size(axis)
    pairs = [(i, i + by) for i in range(count) if 0 <= i + by < count]
    return lax.ppermute(shard, axis, pairs)


def complex_product(first_factor, second_factor, precision=HIGHEST):
    first_real, first_imag = first_factor
    second_real, second_imag = second_factor
    real_real = jnp.matmul(first_real, second_real, precision=precision)
    imag_imag = jnp.matmul(first_imag, second_imag, precision=precision)
    summed = jnp.matmul(
        first_real + first_imag, second_real + second_imag, precision=precision
    )
    return (real_real - imag_imag, summed - real_real - imag_imag)


def newton_product(first_factor, second_factor):
    return complex_product(first_factor, second_factor, HIGHEST)


def first_step_product(first_factor, second_factor):
    return complex_product(first_factor, second_factor, FIRST_STEP_PRECISION)


def part(pair, rows=slice(None), cols=slice(None)):
    return tuple(value[..., rows, cols] for value in pair)


def combine(first_weight, first, second):
    return tuple(first_weight * a - b for a, b in zip(first, second))


def add(first, second):
    return tuple(a + b for a, b in zip(first, second))


def sweep(blocks, guess, coupling_block):
    space_count = lax.axis_size("space")
    size = blocks[0].shape[-1]
    edge = coupling_block[0].shape[-1]
    lead = slice(0, edge)
    trail = slice(size - edge, size)
    adjoint = (jnp.swapaxes(coupling_block[0], -1, -2), -jnp.swapaxes(coupling_block[1], -1, -2))

    def schur_of(incoming):
        return complex_product(complex_product(adjoint, incoming), coupling_block)

    def lead_rows_minus(values, schur, rows):
        update = newton_product(schur, rows)
        return tuple(v.at[..., lead, :].add(-u) for v, u in zip(values, update))

    first = combine(2.0, guess, first_step_product(guess, first_step_product(blocks, guess)))
    left = part(guess, cols=lead)
    right = part(guess, rows=lead)

    applied_trail = newton_product(blocks, part(first, cols=trail))
    boundary = combine(
        2.0, part(first, trail, trail), newton_product(part(first, rows=trail), applied_trail)
    )
    applied_left = newton_product(blocks, left)

    for section in range(1, space_count - 1):
        incoming = from_behind(boundary, "space", 1)
        schur = schur_of(incoming)
        mixed = first_step_product(schur, right)
        mixed_trail = part(mixed, cols=trail)
        step_trail = add(part(first, cols=trail), newton_product(left, mixed_trail))
        step_rows = add(part(first, rows=trail), newton_product(part(left, rows=trail), mixed))
        system_trail = add(applied_trail, newton_product(applied_left, mixed_trail))
        system_trail = lead_rows_minus(system_trail, schur, part(step_trail, rows=lead))
        boundary = combine(
            2.0, part(step_trail, rows=trail), newton_product(step_rows, system_trail)
        )

    applied = newton_product(blocks, first)
    if space_count > 1:
        incoming = from_behind(boundary, "space", 1)
        schur = schur_of(incoming)
        mixed = first_step_product(schur, right)
        step = add(first, newton_product(left, mixed))
        system_step = add(applied, newton_product(applied_left, mixed))
        system_step = lead_rows_minus(system_step, schur, part(step, rows=lead))
    else:
        step = first
        system_step = applied
    return combine(2.0, step, newton_product(step, system_step))


def phonon_matrix(phonon_shift, phonon_strength, momentum_table, energies):
    momenta = momentum_table.shape[0]
    chosen = (
        momentum_table[:, :, None] == jnp.arange(momenta, dtype=jnp.int32)[None, None, :]
    ).astype(jnp.float32)
    momentum_mix = jnp.einsum("kqj,dwq->kjdw", chosen, phonon_strength, precision=HIGHEST)
    energy_rows = jnp.arange(energies, dtype=jnp.int32)
    energy_gap = energy_rows[None, :] - energy_rows[:, None]
    emission = (energy_gap[None, :, :] == -phonon_shift[:, None, None]).astype(jnp.float32)
    absorption = (energy_gap[None, :, :] == phonon_shift[:, None, None]).astype(jnp.float32)
    shift_table = jnp.stack([emission, absorption], axis=0)
    return jnp.einsum("kjdw,dwEF->kjEF", momentum_mix, shift_table, precision=HIGHEST)


def pick_kernel(partner_ref, real_ref, imag_ref, out_ref):
    energy_count, size, _ = real_ref.shape
    chunk = out_ref.shape[2]
    atoms = size // ORB
    per_atom = partner_ref.shape[0] // atoms
    width = per_atom * ORB
    sublanes = 8
    flat = ORB * ORB
    halves = ORB // sublanes

    pick_rows = lax.broadcasted_iota(jnp.int32, (size, width), 0)
    pick_cols = lax.broadcasted_iota(jnp.int32, (size, width), 1)
    row_atom = pick_rows // ORB
    same_orbital = pick_rows % ORB == pick_cols % ORB
    grid_rows = lax.broadcasted_iota(jnp.int32, (sublanes, width), 0)
    grid_cols = lax.broadcasted_iota(jnp.int32, (sublanes, width), 1) // ORB
    diagonal = [(grid_cols - grid_rows) % per_atom == d for d in range(per_atom)]
    lane_tile = lax.broadcasted_iota(jnp.int32, (1, width), 1) // ORB

    def one_atom(atom, carry):
        target = jnp.zeros((1, width), jnp.int32)
        for j in range(per_atom):
            target = jnp.where(lane_tile == j, partner_ref[atom * per_atom + j], target)
        pick = jnp.where((row_atom == target) & same_orbital, 1.0, 0.0).astype(jnp.bfloat16)
        start = pl.multiple_of(atom * ORB, ORB)
        stripes = []
        for e in range(energy_count):
            stripes.append(real_ref[e, pl.ds(start, ORB), :])
            stripes.append(imag_ref[e, pl.ds(start, ORB), :])
        stripes = jnp.concatenate(stripes, axis=0)
        high = stripes.astype(jnp.bfloat16)
        rest = stripes - high.astype(jnp.float32)
        middle = rest.astype(jnp.bfloat16)
        low = (rest - middle.astype(jnp.float32)).astype(jnp.bfloat16)
        pieces = jnp.concatenate([high, middle, low], axis=0)
        selected = jnp.dot(pieces, pick, preferred_element_type=jnp.float32)
        rows = stripes.shape[0]
        chosen = (selected[:rows] + selected[rows : 2 * rows]) + selected[2 * rows :]
        out_start = pl.multiple_of(atom * per_atom, per_atom)
        for g in range(2 * energy_count):
            for half in range(halves):
                row = g * ORB + half * sublanes
                grid = chosen[row : row + sublanes, :]
                flipped = grid
                for d in range(1, per_atom):
                    moved = pltpu.roll(grid, (sublanes - d) % sublanes, 0)
                    moved = pltpu.roll(moved, d * ORB, 1)
                    flipped = jnp.where(diagonal[d], moved, flipped)
                lane = (g % 2) * flat + half * width
                if chunk >= per_atom:
                    out_ref[
                        out_start // chunk, g // 2, pl.ds(out_start % chunk, per_atom), pl.ds(lane, width)
                    ] = flipped
                else:
                    for q in range(per_atom // chunk):
                        out_ref[
                            atom * (per_atom // chunk) + q, g // 2, :, pl.ds(lane, width)
                        ] = flipped[q * chunk : (q + 1) * chunk]
        return carry

    lax.fori_loop(0, atoms, one_atom, 0)


def pick_tiles(green_pair, pair_index, chunks):
    energy_count = green_pair[0].shape[0]
    pair_count = pair_index.shape[0]
    partner = pair_index % ATOMS
    shape = (chunks, energy_count, pair_count // chunks, 2 * ORB * ORB)
    return pl.pallas_call(
        pick_kernel,
        out_shape=jax.ShapeDtypeStruct(shape, jnp.float32),
        in_specs=[
            pl.BlockSpec(memory_space=pltpu.SMEM),
            pl.BlockSpec(memory_space=pltpu.VMEM),
            pl.BlockSpec(memory_space=pltpu.VMEM),
        ],
        out_specs=pl.BlockSpec(memory_space=pltpu.VMEM),
    )(partner, green_pair[0], green_pair[1])


def body(
    blocks, inverse_guess, coupling, pair_index, phonon_shift, phonon_strength, momentum_table
):
    local_blocks = (blocks[:, 0, 0, 0], blocks[:, 0, 0, 1])
    local_guess = (inverse_guess[:, 0, 0, 0], inverse_guess[:, 0, 0, 1])
    coupling_block = (coupling[0, 0, 0], coupling[0, 0, 1])
    energy_count = blocks.shape[0]
    green_pair = sweep(local_blocks, local_guess, coupling_block)
    green_block = jnp.stack(green_pair, axis=1)
    momenta = momentum_table.shape[0]
    energy_groups = lax.axis_size("energy")
    axes = ("energy", "momentum")
    group = energy_groups * lax.axis_size("momentum")
    pair_count = pair_index.shape[1]
    width = 2 * ORB * ORB
    picked = pick_tiles(green_pair, pair_index[0], group)
    mixing = phonon_matrix(
        phonon_shift, phonon_strength, momentum_table, energy_count * energy_groups
    )
    momentum_count = lax.axis_size("momentum")
    chunk = pair_count // group
    staged = picked.reshape(energy_groups, momentum_count, energy_count, chunk, width)
    staged = lax.all_to_all(staged, "momentum", 1, 1, tiled=True)
    arranged = lax.all_to_all(staged, "energy", 0, 0, tiled=True)
    arranged = arranged.reshape(energy_groups, momenta, energy_count, chunk, width)
    mixing_grid = mixing.reshape(
        momenta, momenta, energy_groups, energy_count, energy_groups, energy_count
    )
    summed = jnp.einsum("kjabcd,cjdpx->akbpx", mixing_grid, arranged, precision=HIGHEST)
    summed = summed.reshape(energy_groups, momentum_count, energy_count, chunk, width)
    summed = lax.all_to_all(summed, "momentum", 1, 1, tiled=True)
    summed = lax.all_to_all(summed, "energy", 0, 0, tiled=True)
    self_energy = summed.transpose(2, 0, 1, 3, 4).reshape(energy_count, 1, 1, pair_count, width)
    return (green_block[:, None, None], self_energy)


def solution(mesh):
    return jax.shard_map(
        body,
        mesh=mesh,
        in_specs=(
            P("energy", "momentum", "space", None, None, None),
            P("energy", "momentum", "space", None, None, None),
            P("momentum", "space", None, None, None),
            P("space", None),
            P(),
            P(),
            P(),
        ),
        out_specs=(
            P("energy", "momentum", "space", None, None, None),
            P("energy", "momentum", "space", None, None),
        ),
        check_vma=False,
    )
```

```python
import jax
import jax.numpy as jnp
from jax import lax
from jax.sharding import PartitionSpec as P
from jax.experimental import pallas as pl
from jax.experimental.pallas import tpu as pltpu

ORB = 16
ATOMS = 16
NEWTON = 2


HIGHEST = lax.Precision.HIGHEST
FIRST_STEP_PRECISION = lax.Precision.HIGHEST


def from_behind(shard, axis, by):
    count = lax.axis_size(axis)
    pairs = [(i, i + by) for i in range(count) if 0 <= i + by < count]
    return lax.ppermute(shard, axis, pairs)


def pass_boundary(boundary):
    moved = from_behind(jnp.stack(boundary, axis=0), "space", 1)
    return (moved[0], moved[1])


def complex_product(first_factor, second_factor, precision=HIGHEST):
    first_real, first_imag = first_factor
    second_real, second_imag = second_factor
    real_real = jnp.matmul(first_real, second_real, precision=precision)
    imag_imag = jnp.matmul(first_imag, second_imag, precision=precision)
    summed = jnp.matmul(
        first_real + first_imag, second_real + second_imag, precision=precision
    )
    return (real_real - imag_imag, summed - real_real - imag_imag)


def newton_product(first_factor, second_factor):
    return complex_product(first_factor, second_factor, HIGHEST)


def first_step_product(first_factor, second_factor):
    return complex_product(first_factor, second_factor, FIRST_STEP_PRECISION)


def part(pair, rows=slice(None), cols=slice(None)):
    return tuple(value[..., rows, cols] for value in pair)


def combine(first_weight, first, second):
    return tuple(first_weight * a - b for a, b in zip(first, second))


def add(first, second):
    return tuple(a + b for a, b in zip(first, second))


def sweep(blocks, guess, coupling_block):
    space_count = lax.axis_size("space")
    size = blocks[0].shape[-1]
    edge = coupling_block[0].shape[-1]
    lead = slice(0, edge)
    trail = slice(size - edge, size)
    adjoint = (jnp.swapaxes(coupling_block[0], -1, -2), -jnp.swapaxes(coupling_block[1], -1, -2))

    def schur_of(incoming):
        return complex_product(complex_product(adjoint, incoming), coupling_block)

    def lead_rows_minus(values, schur, rows):
        update = newton_product(schur, rows)
        return tuple(v.at[..., lead, :].add(-u) for v, u in zip(values, update))

    first = combine(2.0, guess, first_step_product(guess, first_step_product(blocks, guess)))
    left = part(guess, cols=lead)
    right = part(guess, rows=lead)

    applied_trail = newton_product(blocks, part(first, cols=trail))
    boundary = combine(
        2.0, part(first, trail, trail), newton_product(part(first, rows=trail), applied_trail)
    )
    applied_left = newton_product(blocks, left)

    for section in range(1, space_count - 1):
        incoming = pass_boundary(boundary)
        schur = schur_of(incoming)
        mixed = first_step_product(schur, right)
        mixed_trail = part(mixed, cols=trail)
        step_trail = add(part(first, cols=trail), newton_product(left, mixed_trail))
        step_rows = add(part(first, rows=trail), newton_product(part(left, rows=trail), mixed))
        system_trail = add(applied_trail, newton_product(applied_left, mixed_trail))
        system_trail = lead_rows_minus(system_trail, schur, part(step_trail, rows=lead))
        boundary = combine(
            2.0, part(step_trail, rows=trail), newton_product(step_rows, system_trail)
        )

    applied = newton_product(blocks, first)
    if space_count > 1:
        incoming = pass_boundary(boundary)
        schur = schur_of(incoming)
        mixed = first_step_product(schur, right)
        step = add(first, newton_product(left, mixed))
        system_step = add(applied, newton_product(applied_left, mixed))
        system_step = lead_rows_minus(system_step, schur, part(step, rows=lead))
    else:
        step = first
        system_step = applied
    return combine(2.0, step, newton_product(step, system_step))


def phonon_matrix(phonon_shift, phonon_strength, momentum_table, energies):
    momenta = momentum_table.shape[0]
    chosen = (
        momentum_table[:, :, None] == jnp.arange(momenta, dtype=jnp.int32)[None, None, :]
    ).astype(jnp.float32)
    momentum_mix = jnp.einsum("kqj,dwq->kjdw", chosen, phonon_strength, precision=HIGHEST)
    energy_rows = jnp.arange(energies, dtype=jnp.int32)
    energy_gap = energy_rows[None, :] - energy_rows[:, None]
    emission = (energy_gap[None, :, :] == -phonon_shift[:, None, None]).astype(jnp.float32)
    absorption = (energy_gap[None, :, :] == phonon_shift[:, None, None]).astype(jnp.float32)
    shift_table = jnp.stack([emission, absorption], axis=0)
    return jnp.einsum("kjdw,dwEF->kjEF", momentum_mix, shift_table, precision=HIGHEST)


def pick_kernel(partner_ref, real_ref, imag_ref, out_ref):
    energy_count, size, _ = real_ref.shape
    chunk = out_ref.shape[2]
    atoms = size // ORB
    per_atom = partner_ref.shape[0] // atoms
    width = per_atom * ORB
    sublanes = 8
    flat = ORB * ORB
    halves = ORB // sublanes

    pick_rows = lax.broadcasted_iota(jnp.int32, (size, width), 0)
    pick_cols = lax.broadcasted_iota(jnp.int32, (size, width), 1)
    row_atom = pick_rows // ORB
    same_orbital = pick_rows % ORB == pick_cols % ORB
    grid_rows = lax.broadcasted_iota(jnp.int32, (sublanes, width), 0)
    grid_cols = lax.broadcasted_iota(jnp.int32, (sublanes, width), 1) // ORB
    diagonal = [(grid_cols - grid_rows) % per_atom == d for d in range(per_atom)]
    lane_tile = lax.broadcasted_iota(jnp.int32, (1, width), 1) // ORB

    def one_atom(atom, carry):
        target = jnp.zeros((1, width), jnp.int32)
        for j in range(per_atom):
            target = jnp.where(lane_tile == j, partner_ref[atom * per_atom + j], target)
        pick = jnp.where((row_atom == target) & same_orbital, 1.0, 0.0).astype(jnp.bfloat16)
        start = pl.multiple_of(atom * ORB, ORB)
        stripes = []
        for e in range(energy_count):
            stripes.append(real_ref[e, pl.ds(start, ORB), :])
            stripes.append(imag_ref[e, pl.ds(start, ORB), :])
        stripes = jnp.concatenate(stripes, axis=0)
        high = stripes.astype(jnp.bfloat16)
        rest = stripes - high.astype(jnp.float32)
        middle = rest.astype(jnp.bfloat16)
        low = (rest - middle.astype(jnp.float32)).astype(jnp.bfloat16)
        pieces = jnp.concatenate([high, middle, low], axis=0)
        selected = jnp.dot(pieces, pick, preferred_element_type=jnp.float32)
        rows = stripes.shape[0]
        chosen = (selected[:rows] + selected[rows : 2 * rows]) + selected[2 * rows :]
        out_start = pl.multiple_of(atom * per_atom, per_atom)
        for g in range(2 * energy_count):
            for half in range(halves):
                row = g * ORB + half * sublanes
                grid = chosen[row : row + sublanes, :]
                flipped = grid
                for d in range(1, per_atom):
                    moved = pltpu.roll(grid, (sublanes - d) % sublanes, 0)
                    moved = pltpu.roll(moved, d * ORB, 1)
                    flipped = jnp.where(diagonal[d], moved, flipped)
                lane = (g % 2) * flat + half * width
                if chunk >= per_atom:
                    out_ref[
                        out_start // chunk, g // 2, pl.ds(out_start % chunk, per_atom), pl.ds(lane, width)
                    ] = flipped
                else:
                    for q in range(per_atom // chunk):
                        out_ref[
                            atom * (per_atom // chunk) + q, g // 2, :, pl.ds(lane, width)
                        ] = flipped[q * chunk : (q + 1) * chunk]
        return carry

    lax.fori_loop(0, atoms, one_atom, 0)


def pick_tiles(green_pair, pair_index, chunks):
    energy_count = green_pair[0].shape[0]
    pair_count = pair_index.shape[0]
    partner = pair_index % ATOMS
    shape = (chunks, energy_count, pair_count // chunks, 2 * ORB * ORB)
    return pl.pallas_call(
        pick_kernel,
        out_shape=jax.ShapeDtypeStruct(shape, jnp.float32),
        in_specs=[
            pl.BlockSpec(memory_space=pltpu.SMEM),
            pl.BlockSpec(memory_space=pltpu.VMEM),
            pl.BlockSpec(memory_space=pltpu.VMEM),
        ],
        out_specs=pl.BlockSpec(memory_space=pltpu.VMEM),
    )(partner, green_pair[0], green_pair[1])


def body(
    blocks, inverse_guess, coupling, pair_index, phonon_shift, phonon_strength, momentum_table
):
    local_blocks = (blocks[:, 0, 0, 0], blocks[:, 0, 0, 1])
    local_guess = (inverse_guess[:, 0, 0, 0], inverse_guess[:, 0, 0, 1])
    coupling_block = (coupling[0, 0, 0], coupling[0, 0, 1])
    energy_count = blocks.shape[0]
    green_pair = sweep(local_blocks, local_guess, coupling_block)
    green_block = jnp.stack(green_pair, axis=1)
    momenta = momentum_table.shape[0]
    energy_groups = lax.axis_size("energy")
    axes = ("energy", "momentum")
    group = energy_groups * lax.axis_size("momentum")
    pair_count = pair_index.shape[1]
    width = 2 * ORB * ORB
    picked = pick_tiles(green_pair, pair_index[0], group)
    mixing = phonon_matrix(
        phonon_shift, phonon_strength, momentum_table, energy_count * energy_groups
    )
    by_pairs = lax.all_to_all(picked, axes, 0, 0, tiled=True)
    arranged = by_pairs.reshape(energy_groups, momenta, energy_count, pair_count // group, width)
    mixing_grid = mixing.reshape(
        momenta, momenta, energy_groups, energy_count, energy_groups, energy_count
    )
    summed = jnp.einsum("kjabcd,cjdpx->akbpx", mixing_grid, arranged, precision=HIGHEST)
    summed = summed.reshape(group, energy_count, pair_count // group, width)
    self_energy = lax.all_to_all(summed, axes, 0, 2, tiled=True)
    self_energy = self_energy.reshape(energy_count, 1, 1, pair_count, width)
    return (green_block[:, None, None], self_energy)


def solution(mesh):
    return jax.shard_map(
        body,
        mesh=mesh,
        in_specs=(
            P("energy", "momentum", "space", None, None, None),
            P("energy", "momentum", "space", None, None, None),
            P("momentum", "space", None, None, None),
            P("space", None),
            P(),
            P(),
            P(),
        ),
        out_specs=(
            P("energy", "momentum", "space", None, None, None),
            P("energy", "momentum", "space", None, None),
        ),
        check_vma=False,
    )
```

```python
import jax
import jax.numpy as jnp
from jax import lax
from jax.sharding import PartitionSpec as P
from jax.experimental import pallas as pl
from jax.experimental.pallas import tpu as pltpu

ORB = 16
ATOMS = 16
NEWTON = 2


HIGHEST = lax.Precision.HIGHEST
FIRST_STEP_PRECISION = lax.Precision.HIGHEST


def from_behind(shard, axis, by):
    count = lax.axis_size(axis)
    pairs = [(i, i + by) for i in range(count) if 0 <= i + by < count]
    return lax.ppermute(shard, axis, pairs)


def pass_boundary(boundary):
    moved = from_behind(jnp.stack(boundary, axis=0), "space", 1)
    return (moved[0], moved[1])


def complex_product(first_factor, second_factor, precision=HIGHEST):
    first_real, first_imag = first_factor
    second_real, second_imag = second_factor
    real_real = jnp.matmul(first_real, second_real, precision=precision)
    imag_imag = jnp.matmul(first_imag, second_imag, precision=precision)
    summed = jnp.matmul(
        first_real + first_imag, second_real + second_imag, precision=precision
    )
    return (real_real - imag_imag, summed - real_real - imag_imag)


def newton_product(first_factor, second_factor):
    return complex_product(first_factor, second_factor, HIGHEST)


def first_step_product(first_factor, second_factor):
    return complex_product(first_factor, second_factor, FIRST_STEP_PRECISION)


def part(pair, rows=slice(None), cols=slice(None)):
    return tuple(value[..., rows, cols] for value in pair)


def combine(first_weight, first, second):
    return tuple(first_weight * a - b for a, b in zip(first, second))


def add(first, second):
    return tuple(a + b for a, b in zip(first, second))


def sweep(blocks, guess, coupling_block):
    space_count = lax.axis_size("space")
    size = blocks[0].shape[-1]
    edge = coupling_block[0].shape[-1]
    lead = slice(0, edge)
    trail = slice(size - edge, size)
    adjoint = (jnp.swapaxes(coupling_block[0], -1, -2), -jnp.swapaxes(coupling_block[1], -1, -2))

    def schur_of(incoming):
        return complex_product(complex_product(adjoint, incoming), coupling_block)

    def lead_rows_minus(values, schur, rows):
        update = newton_product(schur, rows)
        return tuple(v.at[..., lead, :].add(-u) for v, u in zip(values, update))

    first = combine(2.0, guess, first_step_product(guess, first_step_product(blocks, guess)))
    left = part(guess, cols=lead)
    right = part(guess, rows=lead)

    applied_trail = newton_product(blocks, part(first, cols=trail))
    boundary = combine(
        2.0, part(first, trail, trail), newton_product(part(first, rows=trail), applied_trail)
    )
    applied_left = newton_product(blocks, left)

    for section in range(1, space_count - 1):
        incoming = pass_boundary(boundary)
        schur = schur_of(incoming)
        mixed = first_step_product(schur, right)
        mixed_trail = part(mixed, cols=trail)
        step_trail = add(part(first, cols=trail), newton_product(left, mixed_trail))
        step_rows = add(part(first, rows=trail), newton_product(part(left, rows=trail), mixed))
        system_trail = add(applied_trail, newton_product(applied_left, mixed_trail))
        system_trail = lead_rows_minus(system_trail, schur, part(step_trail, rows=lead))
        boundary = combine(
            2.0, part(step_trail, rows=trail), newton_product(step_rows, system_trail)
        )

    applied = newton_product(blocks, first)
    stacked_left = tuple(jnp.concatenate(pair, axis=-2) for pair in zip(left, applied_left))
    if space_count > 1:
        incoming = pass_boundary(boundary)
        schur = schur_of(incoming)
        mixed = first_step_product(schur, right)
        both = newton_product(stacked_left, mixed)
        step = add(first, part(both, rows=slice(0, size)))
        system_step = add(applied, part(both, rows=slice(size, 2 * size)))
        system_step = lead_rows_minus(system_step, schur, part(step, rows=lead))
    else:
        step = first
        system_step = applied
    return combine(2.0, step, newton_product(step, system_step))


def phonon_matrix(phonon_shift, phonon_strength, momentum_table, energies):
    momenta = momentum_table.shape[0]
    chosen = (
        momentum_table[:, :, None] == jnp.arange(momenta, dtype=jnp.int32)[None, None, :]
    ).astype(jnp.float32)
    momentum_mix = jnp.einsum("kqj,dwq->kjdw", chosen, phonon_strength, precision=HIGHEST)
    energy_rows = jnp.arange(energies, dtype=jnp.int32)
    energy_gap = energy_rows[None, :] - energy_rows[:, None]
    emission = (energy_gap[None, :, :] == -phonon_shift[:, None, None]).astype(jnp.float32)
    absorption = (energy_gap[None, :, :] == phonon_shift[:, None, None]).astype(jnp.float32)
    shift_table = jnp.stack([emission, absorption], axis=0)
    return jnp.einsum("kjdw,dwEF->kjEF", momentum_mix, shift_table, precision=HIGHEST)


def pick_kernel(partner_ref, real_ref, imag_ref, out_ref):
    energy_count, size, _ = real_ref.shape
    chunk = out_ref.shape[2]
    atoms = size // ORB
    per_atom = partner_ref.shape[0] // atoms
    width = per_atom * ORB
    sublanes = 8
    flat = ORB * ORB
    halves = ORB // sublanes

    pick_rows = lax.broadcasted_iota(jnp.int32, (size, width), 0)
    pick_cols = lax.broadcasted_iota(jnp.int32, (size, width), 1)
    row_atom = pick_rows // ORB
    same_orbital = pick_rows % ORB == pick_cols % ORB
    grid_rows = lax.broadcasted_iota(jnp.int32, (sublanes, width), 0)
    grid_cols = lax.broadcasted_iota(jnp.int32, (sublanes, width), 1) // ORB
    diagonal = [(grid_cols - grid_rows) % per_atom == d for d in range(per_atom)]
    lane_tile = lax.broadcasted_iota(jnp.int32, (1, width), 1) // ORB

    def one_atom(atom, carry):
        target = jnp.zeros((1, width), jnp.int32)
        for j in range(per_atom):
            target = jnp.where(lane_tile == j, partner_ref[atom * per_atom + j], target)
        pick = jnp.where((row_atom == target) & same_orbital, 1.0, 0.0).astype(jnp.bfloat16)
        start = pl.multiple_of(atom * ORB, ORB)
        stripes = []
        for e in range(energy_count):
            stripes.append(real_ref[e, pl.ds(start, ORB), :])
            stripes.append(imag_ref[e, pl.ds(start, ORB), :])
        stripes = jnp.concatenate(stripes, axis=0)
        high = stripes.astype(jnp.bfloat16)
        rest = stripes - high.astype(jnp.float32)
        middle = rest.astype(jnp.bfloat16)
        low = (rest - middle.astype(jnp.float32)).astype(jnp.bfloat16)
        pieces = jnp.concatenate([high, middle, low], axis=0)
        selected = jnp.dot(pieces, pick, preferred_element_type=jnp.float32)
        rows = stripes.shape[0]
        chosen = (selected[:rows] + selected[rows : 2 * rows]) + selected[2 * rows :]
        out_start = pl.multiple_of(atom * per_atom, per_atom)
        for g in range(2 * energy_count):
            for half in range(halves):
                row = g * ORB + half * sublanes
                grid = chosen[row : row + sublanes, :]
                flipped = grid
                for d in range(1, per_atom):
                    moved = pltpu.roll(grid, (sublanes - d) % sublanes, 0)
                    moved = pltpu.roll(moved, d * ORB, 1)
                    flipped = jnp.where(diagonal[d], moved, flipped)
                lane = (g % 2) * flat + half * width
                if chunk >= per_atom:
                    out_ref[
                        out_start // chunk, g // 2, pl.ds(out_start % chunk, per_atom), pl.ds(lane, width)
                    ] = flipped
                else:
                    for q in range(per_atom // chunk):
                        out_ref[
                            atom * (per_atom // chunk) + q, g // 2, :, pl.ds(lane, width)
                        ] = flipped[q * chunk : (q + 1) * chunk]
        return carry

    lax.fori_loop(0, atoms, one_atom, 0)


def pick_tiles(green_pair, pair_index, chunks):
    energy_count = green_pair[0].shape[0]
    pair_count = pair_index.shape[0]
    partner = pair_index % ATOMS
    shape = (chunks, energy_count, pair_count // chunks, 2 * ORB * ORB)
    return pl.pallas_call(
        pick_kernel,
        out_shape=jax.ShapeDtypeStruct(shape, jnp.float32),
        in_specs=[
            pl.BlockSpec(memory_space=pltpu.SMEM),
            pl.BlockSpec(memory_space=pltpu.VMEM),
            pl.BlockSpec(memory_space=pltpu.VMEM),
        ],
        out_specs=pl.BlockSpec(memory_space=pltpu.VMEM),
    )(partner, green_pair[0], green_pair[1])


def body(
    blocks, inverse_guess, coupling, pair_index, phonon_shift, phonon_strength, momentum_table
):
    local_blocks = (blocks[:, 0, 0, 0], blocks[:, 0, 0, 1])
    local_guess = (inverse_guess[:, 0, 0, 0], inverse_guess[:, 0, 0, 1])
    coupling_block = (coupling[0, 0, 0], coupling[0, 0, 1])
    energy_count = blocks.shape[0]
    green_pair = sweep(local_blocks, local_guess, coupling_block)
    green_block = jnp.stack(green_pair, axis=1)
    momenta = momentum_table.shape[0]
    energy_groups = lax.axis_size("energy")
    axes = ("energy", "momentum")
    group = energy_groups * lax.axis_size("momentum")
    pair_count = pair_index.shape[1]
    width = 2 * ORB * ORB
    picked = pick_tiles(green_pair, pair_index[0], group)
    mixing = phonon_matrix(
        phonon_shift, phonon_strength, momentum_table, energy_count * energy_groups
    )
    by_pairs = lax.all_to_all(picked, axes, 0, 0, tiled=True)
    arranged = by_pairs.reshape(energy_groups, momenta, energy_count, pair_count // group, width)
    mixing_grid = mixing.reshape(
        momenta, momenta, energy_groups, energy_count, energy_groups, energy_count
    )
    summed = jnp.einsum("kjabcd,cjdpx->akbpx", mixing_grid, arranged, precision=HIGHEST)
    summed = summed.reshape(group, energy_count, pair_count // group, width)
    self_energy = lax.all_to_all(summed, axes, 0, 2, tiled=True)
    self_energy = self_energy.reshape(energy_count, 1, 1, pair_count, width)
    return (green_block[:, None, None], self_energy)


def solution(mesh):
    return jax.shard_map(
        body,
        mesh=mesh,
        in_specs=(
            P("energy", "momentum", "space", None, None, None),
            P("energy", "momentum", "space", None, None, None),
            P("momentum", "space", None, None, None),
            P("space", None),
            P(),
            P(),
            P(),
        ),
        out_specs=(
            P("energy", "momentum", "space", None, None, None),
            P("energy", "momentum", "space", None, None),
        ),
        check_vma=False,
    )
```

```python
import jax
import jax.numpy as jnp
from jax import lax
from jax.sharding import PartitionSpec as P
from jax.experimental import pallas as pl
from jax.experimental.pallas import tpu as pltpu

ORB = 16
ATOMS = 16
NEWTON = 2


HIGHEST = lax.Precision.HIGHEST
FIRST_STEP_PRECISION = lax.Precision.HIGHEST


def from_behind(shard, axis, by):
    count = lax.axis_size(axis)
    pairs = [(i, i + by) for i in range(count) if 0 <= i + by < count]
    return lax.ppermute(shard, axis, pairs)


def pass_boundary(boundary):
    moved = from_behind(jnp.stack(boundary, axis=0), "space", 1)
    return (moved[0], moved[1])


def complex_product(first_factor, second_factor, precision=HIGHEST):
    first_real, first_imag = first_factor
    second_real, second_imag = second_factor
    real_real = jnp.matmul(first_real, second_real, precision=precision)
    imag_imag = jnp.matmul(first_imag, second_imag, precision=precision)
    summed = jnp.matmul(
        first_real + first_imag, second_real + second_imag, precision=precision
    )
    return (real_real - imag_imag, summed - real_real - imag_imag)


def newton_product(first_factor, second_factor):
    return complex_product(first_factor, second_factor, HIGHEST)


def first_step_product(first_factor, second_factor):
    return complex_product(first_factor, second_factor, FIRST_STEP_PRECISION)


def part(pair, rows=slice(None), cols=slice(None)):
    return tuple(value[..., rows, cols] for value in pair)


def combine(first_weight, first, second):
    return tuple(first_weight * a - b for a, b in zip(first, second))


def add(first, second):
    return tuple(a + b for a, b in zip(first, second))


def sweep(blocks, guess, coupling_block):
    space_count = lax.axis_size("space")
    size = blocks[0].shape[-1]
    edge = coupling_block[0].shape[-1]
    lead = slice(0, edge)
    trail = slice(size - edge, size)
    adjoint = (jnp.swapaxes(coupling_block[0], -1, -2), -jnp.swapaxes(coupling_block[1], -1, -2))

    def schur_of(incoming):
        return complex_product(complex_product(adjoint, incoming), coupling_block)

    def lead_rows_minus(values, schur, rows):
        update = newton_product(schur, rows)
        return tuple(v.at[..., lead, :].add(-u) for v, u in zip(values, update))

    applied_guess = first_step_product(blocks, guess)
    first = combine(2.0, guess, first_step_product(guess, applied_guess))
    left = part(guess, cols=lead)
    right = part(guess, rows=lead)

    applied_trail = newton_product(blocks, part(first, cols=trail))
    boundary = combine(
        2.0, part(first, trail, trail), newton_product(part(first, rows=trail), applied_trail)
    )
    applied_left = part(applied_guess, cols=lead)

    for section in range(1, space_count - 1):
        incoming = pass_boundary(boundary)
        schur = schur_of(incoming)
        mixed = first_step_product(schur, right)
        mixed_trail = part(mixed, cols=trail)
        step_trail = add(part(first, cols=trail), newton_product(left, mixed_trail))
        step_rows = add(part(first, rows=trail), newton_product(part(left, rows=trail), mixed))
        system_trail = add(applied_trail, newton_product(applied_left, mixed_trail))
        system_trail = lead_rows_minus(system_trail, schur, part(step_trail, rows=lead))
        boundary = combine(
            2.0, part(step_trail, rows=trail), newton_product(step_rows, system_trail)
        )

    applied = newton_product(blocks, first)
    stacked_left = tuple(jnp.concatenate(pair, axis=-2) for pair in zip(left, applied_left))
    if space_count > 1:
        incoming = pass_boundary(boundary)
        schur = schur_of(incoming)
        mixed = first_step_product(schur, right)
        both = newton_product(stacked_left, mixed)
        step = add(first, part(both, rows=slice(0, size)))
        system_step = add(applied, part(both, rows=slice(size, 2 * size)))
        system_step = lead_rows_minus(system_step, schur, part(step, rows=lead))
    else:
        step = first
        system_step = applied
    return combine(2.0, step, newton_product(step, system_step))


def phonon_matrix(phonon_shift, phonon_strength, momentum_table, energies):
    momenta = momentum_table.shape[0]
    chosen = (
        momentum_table[:, :, None] == jnp.arange(momenta, dtype=jnp.int32)[None, None, :]
    ).astype(jnp.float32)
    momentum_mix = jnp.einsum("kqj,dwq->kjdw", chosen, phonon_strength, precision=HIGHEST)
    energy_rows = jnp.arange(energies, dtype=jnp.int32)
    energy_gap = energy_rows[None, :] - energy_rows[:, None]
    emission = (energy_gap[None, :, :] == -phonon_shift[:, None, None]).astype(jnp.float32)
    absorption = (energy_gap[None, :, :] == phonon_shift[:, None, None]).astype(jnp.float32)
    shift_table = jnp.stack([emission, absorption], axis=0)
    return jnp.einsum("kjdw,dwEF->kjEF", momentum_mix, shift_table, precision=HIGHEST)


def pick_kernel(partner_ref, real_ref, imag_ref, out_ref):
    energy_count, size, _ = real_ref.shape
    chunk = out_ref.shape[2]
    atoms = size // ORB
    per_atom = partner_ref.shape[0] // atoms
    width = per_atom * ORB
    sublanes = 8
    flat = ORB * ORB
    halves = ORB // sublanes

    pick_rows = lax.broadcasted_iota(jnp.int32, (size, width), 0)
    pick_cols = lax.broadcasted_iota(jnp.int32, (size, width), 1)
    row_atom = pick_rows // ORB
    same_orbital = pick_rows % ORB == pick_cols % ORB
    grid_rows = lax.broadcasted_iota(jnp.int32, (sublanes, width), 0)
    grid_cols = lax.broadcasted_iota(jnp.int32, (sublanes, width), 1) // ORB
    diagonal = [(grid_cols - grid_rows) % per_atom == d for d in range(per_atom)]
    lane_tile = lax.broadcasted_iota(jnp.int32, (1, width), 1) // ORB

    def one_atom(atom, carry):
        target = jnp.zeros((1, width), jnp.int32)
        for j in range(per_atom):
            target = jnp.where(lane_tile == j, partner_ref[atom * per_atom + j], target)
        pick = jnp.where((row_atom == target) & same_orbital, 1.0, 0.0).astype(jnp.bfloat16)
        start = pl.multiple_of(atom * ORB, ORB)
        stripes = []
        for e in range(energy_count):
            stripes.append(real_ref[e, pl.ds(start, ORB), :])
            stripes.append(imag_ref[e, pl.ds(start, ORB), :])
        stripes = jnp.concatenate(stripes, axis=0)
        high = stripes.astype(jnp.bfloat16)
        rest = stripes - high.astype(jnp.float32)
        middle = rest.astype(jnp.bfloat16)
        low = (rest - middle.astype(jnp.float32)).astype(jnp.bfloat16)
        pieces = jnp.concatenate([high, middle, low], axis=0)
        selected = jnp.dot(pieces, pick, preferred_element_type=jnp.float32)
        rows = stripes.shape[0]
        chosen = (selected[:rows] + selected[rows : 2 * rows]) + selected[2 * rows :]
        out_start = pl.multiple_of(atom * per_atom, per_atom)
        for g in range(2 * energy_count):
            for half in range(halves):
                row = g * ORB + half * sublanes
                grid = chosen[row : row + sublanes, :]
                flipped = grid
                for d in range(1, per_atom):
                    moved = pltpu.roll(grid, (sublanes - d) % sublanes, 0)
                    moved = pltpu.roll(moved, d * ORB, 1)
                    flipped = jnp.where(diagonal[d], moved, flipped)
                lane = (g % 2) * flat + half * width
                if chunk >= per_atom:
                    out_ref[
                        out_start // chunk, g // 2, pl.ds(out_start % chunk, per_atom), pl.ds(lane, width)
                    ] = flipped
                else:
                    for q in range(per_atom // chunk):
                        out_ref[
                            atom * (per_atom // chunk) + q, g // 2, :, pl.ds(lane, width)
                        ] = flipped[q * chunk : (q + 1) * chunk]
        return carry

    lax.fori_loop(0, atoms, one_atom, 0)


def pick_tiles(green_pair, pair_index, chunks):
    energy_count = green_pair[0].shape[0]
    pair_count = pair_index.shape[0]
    partner = pair_index % ATOMS
    shape = (chunks, energy_count, pair_count // chunks, 2 * ORB * ORB)
    return pl.pallas_call(
        pick_kernel,
        out_shape=jax.ShapeDtypeStruct(shape, jnp.float32),
        in_specs=[
            pl.BlockSpec(memory_space=pltpu.SMEM),
            pl.BlockSpec(memory_space=pltpu.VMEM),
            pl.BlockSpec(memory_space=pltpu.VMEM),
        ],
        out_specs=pl.BlockSpec(memory_space=pltpu.VMEM),
    )(partner, green_pair[0], green_pair[1])


def body(
    blocks, inverse_guess, coupling, pair_index, phonon_shift, phonon_strength, momentum_table
):
    local_blocks = (blocks[:, 0, 0, 0], blocks[:, 0, 0, 1])
    local_guess = (inverse_guess[:, 0, 0, 0], inverse_guess[:, 0, 0, 1])
    coupling_block = (coupling[0, 0, 0], coupling[0, 0, 1])
    energy_count = blocks.shape[0]
    green_pair = sweep(local_blocks, local_guess, coupling_block)
    green_block = jnp.stack(green_pair, axis=1)
    momenta = momentum_table.shape[0]
    energy_groups = lax.axis_size("energy")
    axes = ("energy", "momentum")
    group = energy_groups * lax.axis_size("momentum")
    pair_count = pair_index.shape[1]
    width = 2 * ORB * ORB
    picked = pick_tiles(green_pair, pair_index[0], group)
    mixing = phonon_matrix(
        phonon_shift, phonon_strength, momentum_table, energy_count * energy_groups
    )
    by_pairs = lax.all_to_all(picked, axes, 0, 0, tiled=True)
    arranged = by_pairs.reshape(energy_groups, momenta, energy_count, pair_count // group, width)
    mixing_grid = mixing.reshape(
        momenta, momenta, energy_groups, energy_count, energy_groups, energy_count
    )
    summed = jnp.einsum("kjabcd,cjdpx->akbpx", mixing_grid, arranged, precision=HIGHEST)
    summed = summed.reshape(group, energy_count, pair_count // group, width)
    self_energy = lax.all_to_all(summed, axes, 0, 2, tiled=True)
    self_energy = self_energy.reshape(energy_count, 1, 1, pair_count, width)
    return (green_block[:, None, None], self_energy)


def solution(mesh):
    return jax.shard_map(
        body,
        mesh=mesh,
        in_specs=(
            P("energy", "momentum", "space", None, None, None),
            P("energy", "momentum", "space", None, None, None),
            P("momentum", "space", None, None, None),
            P("space", None),
            P(),
            P(),
            P(),
        ),
        out_specs=(
            P("energy", "momentum", "space", None, None, None),
            P("energy", "momentum", "space", None, None),
        ),
        check_vma=False,
    )
```

```python
import jax
import jax.numpy as jnp
from jax import lax
from jax.sharding import PartitionSpec as P
from jax.experimental import pallas as pl
from jax.experimental.pallas import tpu as pltpu

ORB = 16
ATOMS = 16
NEWTON = 2


HIGHEST = lax.Precision.HIGHEST
FIRST_STEP_PRECISION = lax.Precision.HIGHEST


def from_behind(shard, axis, by):
    count = lax.axis_size(axis)
    pairs = [(i, i + by) for i in range(count) if 0 <= i + by < count]
    return lax.ppermute(shard, axis, pairs)


def pass_boundary(boundary):
    moved = from_behind(jnp.stack(boundary, axis=0), "space", 1)
    return (moved[0], moved[1])


def complex_product(first_factor, second_factor, precision=HIGHEST):
    first_real, first_imag = first_factor
    second_real, second_imag = second_factor
    real_real = jnp.matmul(first_real, second_real, precision=precision)
    imag_imag = jnp.matmul(first_imag, second_imag, precision=precision)
    summed = jnp.matmul(
        first_real + first_imag, second_real + second_imag, precision=precision
    )
    return (real_real - imag_imag, summed - real_real - imag_imag)


def newton_product(first_factor, second_factor):
    return complex_product(first_factor, second_factor, HIGHEST)


def first_step_product(first_factor, second_factor):
    return complex_product(first_factor, second_factor, FIRST_STEP_PRECISION)


def part(pair, rows=slice(None), cols=slice(None)):
    return tuple(value[..., rows, cols] for value in pair)


def combine(first_weight, first, second):
    return tuple(first_weight * a - b for a, b in zip(first, second))


def add(first, second):
    return tuple(a + b for a, b in zip(first, second))


def sweep(blocks, guess, coupling_block):
    space_count = lax.axis_size("space")
    size = blocks[0].shape[-1]
    edge = coupling_block[0].shape[-1]
    lead = slice(0, edge)
    trail = slice(size - edge, size)
    adjoint = (jnp.swapaxes(coupling_block[0], -1, -2), -jnp.swapaxes(coupling_block[1], -1, -2))

    def schur_of(incoming):
        return complex_product(complex_product(adjoint, incoming), coupling_block)

    def lead_rows_minus(values, schur, rows):
        update = newton_product(schur, rows)
        return tuple(v.at[..., lead, :].add(-u) for v, u in zip(values, update))

    applied_guess = first_step_product(blocks, guess)
    first = combine(2.0, guess, first_step_product(guess, applied_guess))
    left = part(guess, cols=lead)
    right = part(guess, rows=lead)

    applied_trail = newton_product(blocks, part(first, cols=trail))
    boundary = combine(
        2.0, part(first, trail, trail), newton_product(part(first, rows=trail), applied_trail)
    )
    applied_left = part(applied_guess, cols=lead)

    for section in range(1, space_count - 1):
        incoming = pass_boundary(boundary)
        schur = schur_of(incoming)
        mixed = first_step_product(schur, right)
        mixed_trail = part(mixed, cols=trail)
        step_trail = add(part(first, cols=trail), newton_product(left, mixed_trail))
        step_rows = add(part(first, rows=trail), newton_product(part(left, rows=trail), mixed))
        system_trail = add(applied_trail, newton_product(applied_left, mixed_trail))
        system_trail = lead_rows_minus(system_trail, schur, part(step_trail, rows=lead))
        boundary = combine(
            2.0, part(step_trail, rows=trail), newton_product(step_rows, system_trail)
        )

    applied_lead = newton_product(blocks, part(first, cols=slice(0, size - edge)))
    applied = tuple(jnp.concatenate(pair, axis=-1) for pair in zip(applied_lead, applied_trail))
    stacked_left = tuple(jnp.concatenate(pair, axis=-2) for pair in zip(left, applied_left))
    if space_count > 1:
        incoming = pass_boundary(boundary)
        schur = schur_of(incoming)
        mixed = first_step_product(schur, right)
        both = newton_product(stacked_left, mixed)
        step = add(first, part(both, rows=slice(0, size)))
        system_step = add(applied, part(both, rows=slice(size, 2 * size)))
        system_step = lead_rows_minus(system_step, schur, part(step, rows=lead))
    else:
        step = first
        system_step = applied
    return combine(2.0, step, newton_product(step, system_step))


def phonon_matrix(phonon_shift, phonon_strength, momentum_table, energies):
    momenta = momentum_table.shape[0]
    chosen = (
        momentum_table[:, :, None] == jnp.arange(momenta, dtype=jnp.int32)[None, None, :]
    ).astype(jnp.float32)
    momentum_mix = jnp.einsum("kqj,dwq->kjdw", chosen, phonon_strength, precision=HIGHEST)
    energy_rows = jnp.arange(energies, dtype=jnp.int32)
    energy_gap = energy_rows[None, :] - energy_rows[:, None]
    emission = (energy_gap[None, :, :] == -phonon_shift[:, None, None]).astype(jnp.float32)
    absorption = (energy_gap[None, :, :] == phonon_shift[:, None, None]).astype(jnp.float32)
    shift_table = jnp.stack([emission, absorption], axis=0)
    return jnp.einsum("kjdw,dwEF->kjEF", momentum_mix, shift_table, precision=HIGHEST)


def pick_kernel(partner_ref, real_ref, imag_ref, out_ref):
    energy_count, size, _ = real_ref.shape
    chunk = out_ref.shape[2]
    atoms = size // ORB
    per_atom = partner_ref.shape[0] // atoms
    width = per_atom * ORB
    sublanes = 8
    flat = ORB * ORB
    halves = ORB // sublanes

    pick_rows = lax.broadcasted_iota(jnp.int32, (size, width), 0)
    pick_cols = lax.broadcasted_iota(jnp.int32, (size, width), 1)
    row_atom = pick_rows // ORB
    same_orbital = pick_rows % ORB == pick_cols % ORB
    grid_rows = lax.broadcasted_iota(jnp.int32, (sublanes, width), 0)
    grid_cols = lax.broadcasted_iota(jnp.int32, (sublanes, width), 1) // ORB
    diagonal = [(grid_cols - grid_rows) % per_atom == d for d in range(per_atom)]
    lane_tile = lax.broadcasted_iota(jnp.int32, (1, width), 1) // ORB

    def one_atom(atom, carry):
        target = jnp.zeros((1, width), jnp.int32)
        for j in range(per_atom):
            target = jnp.where(lane_tile == j, partner_ref[atom * per_atom + j], target)
        pick = jnp.where((row_atom == target) & same_orbital, 1.0, 0.0).astype(jnp.bfloat16)
        start = pl.multiple_of(atom * ORB, ORB)
        stripes = []
        for e in range(energy_count):
            stripes.append(real_ref[e, pl.ds(start, ORB), :])
            stripes.append(imag_ref[e, pl.ds(start, ORB), :])
        stripes = jnp.concatenate(stripes, axis=0)
        high = stripes.astype(jnp.bfloat16)
        rest = stripes - high.astype(jnp.float32)
        middle = rest.astype(jnp.bfloat16)
        low = (rest - middle.astype(jnp.float32)).astype(jnp.bfloat16)
        pieces = jnp.concatenate([high, middle, low], axis=0)
        selected = jnp.dot(pieces, pick, preferred_element_type=jnp.float32)
        rows = stripes.shape[0]
        chosen = (selected[:rows] + selected[rows : 2 * rows]) + selected[2 * rows :]
        out_start = pl.multiple_of(atom * per_atom, per_atom)
        for g in range(2 * energy_count):
            for half in range(halves):
                row = g * ORB + half * sublanes
                grid = chosen[row : row + sublanes, :]
                flipped = grid
                for d in range(1, per_atom):
                    moved = pltpu.roll(grid, (sublanes - d) % sublanes, 0)
                    moved = pltpu.roll(moved, d * ORB, 1)
                    flipped = jnp.where(diagonal[d], moved, flipped)
                lane = (g % 2) * flat + half * width
                if chunk >= per_atom:
                    out_ref[
                        out_start // chunk, g // 2, pl.ds(out_start % chunk, per_atom), pl.ds(lane, width)
                    ] = flipped
                else:
                    for q in range(per_atom // chunk):
                        out_ref[
                            atom * (per_atom // chunk) + q, g // 2, :, pl.ds(lane, width)
                        ] = flipped[q * chunk : (q + 1) * chunk]
        return carry

    lax.fori_loop(0, atoms, one_atom, 0)


def pick_tiles(green_pair, pair_index, chunks):
    energy_count = green_pair[0].shape[0]
    pair_count = pair_index.shape[0]
    partner = pair_index % ATOMS
    shape = (chunks, energy_count, pair_count // chunks, 2 * ORB * ORB)
    return pl.pallas_call(
        pick_kernel,
        out_shape=jax.ShapeDtypeStruct(shape, jnp.float32),
        in_specs=[
            pl.BlockSpec(memory_space=pltpu.SMEM),
            pl.BlockSpec(memory_space=pltpu.VMEM),
            pl.BlockSpec(memory_space=pltpu.VMEM),
        ],
        out_specs=pl.BlockSpec(memory_space=pltpu.VMEM),
    )(partner, green_pair[0], green_pair[1])


def body(
    blocks, inverse_guess, coupling, pair_index, phonon_shift, phonon_strength, momentum_table
):
    local_blocks = (blocks[:, 0, 0, 0], blocks[:, 0, 0, 1])
    local_guess = (inverse_guess[:, 0, 0, 0], inverse_guess[:, 0, 0, 1])
    coupling_block = (coupling[0, 0, 0], coupling[0, 0, 1])
    energy_count = blocks.shape[0]
    green_pair = sweep(local_blocks, local_guess, coupling_block)
    green_block = jnp.stack(green_pair, axis=1)
    momenta = momentum_table.shape[0]
    energy_groups = lax.axis_size("energy")
    axes = ("energy", "momentum")
    group = energy_groups * lax.axis_size("momentum")
    pair_count = pair_index.shape[1]
    width = 2 * ORB * ORB
    picked = pick_tiles(green_pair, pair_index[0], group)
    mixing = phonon_matrix(
        phonon_shift, phonon_strength, momentum_table, energy_count * energy_groups
    )
    by_pairs = lax.all_to_all(picked, axes, 0, 0, tiled=True)
    arranged = by_pairs.reshape(energy_groups, momenta, energy_count, pair_count // group, width)
    mixing_grid = mixing.reshape(
        momenta, momenta, energy_groups, energy_count, energy_groups, energy_count
    )
    summed = jnp.einsum("kjabcd,cjdpx->akbpx", mixing_grid, arranged, precision=HIGHEST)
    summed = summed.reshape(group, energy_count, pair_count // group, width)
    self_energy = lax.all_to_all(summed, axes, 0, 2, tiled=True)
    self_energy = self_energy.reshape(energy_count, 1, 1, pair_count, width)
    return (green_block[:, None, None], self_energy)


def solution(mesh):
    return jax.shard_map(
        body,
        mesh=mesh,
        in_specs=(
            P("energy", "momentum", "space", None, None, None),
            P("energy", "momentum", "space", None, None, None),
            P("momentum", "space", None, None, None),
            P("space", None),
            P(),
            P(),
            P(),
        ),
        out_specs=(
            P("energy", "momentum", "space", None, None, None),
            P("energy", "momentum", "space", None, None),
        ),
        check_vma=False,
    )
```

```python
import jax
import jax.numpy as jnp
from jax import lax
from jax.sharding import PartitionSpec as P
from jax.experimental import pallas as pl
from jax.experimental.pallas import tpu as pltpu

ORB = 16
ATOMS = 16
NEWTON = 2


HIGHEST = lax.Precision.HIGHEST
FIRST_STEP_PRECISION = lax.Precision.HIGHEST


def from_behind(shard, axis, by):
    count = lax.axis_size(axis)
    pairs = [(i, i + by) for i in range(count) if 0 <= i + by < count]
    return lax.ppermute(shard, axis, pairs)


def pass_boundary(boundary):
    moved = from_behind(jnp.stack(boundary, axis=0), "space", 1)
    return (moved[0], moved[1])


def complex_product(first_factor, second_factor, precision=HIGHEST):
    first_real, first_imag = first_factor
    second_real, second_imag = second_factor
    real_real = jnp.matmul(first_real, second_real, precision=precision)
    imag_imag = jnp.matmul(first_imag, second_imag, precision=precision)
    summed = jnp.matmul(
        first_real + first_imag, second_real + second_imag, precision=precision
    )
    return (real_real - imag_imag, summed - real_real - imag_imag)


def newton_product(first_factor, second_factor):
    return complex_product(first_factor, second_factor, HIGHEST)


def first_step_product(first_factor, second_factor):
    return complex_product(first_factor, second_factor, FIRST_STEP_PRECISION)


def part(pair, rows=slice(None), cols=slice(None)):
    return tuple(value[..., rows, cols] for value in pair)


def combine(first_weight, first, second):
    return tuple(first_weight * a - b for a, b in zip(first, second))


def add(first, second):
    return tuple(a + b for a, b in zip(first, second))


def sweep(blocks, guess, coupling_block):
    space_count = lax.axis_size("space")
    size = blocks[0].shape[-1]
    edge = coupling_block[0].shape[-1]
    lead = slice(0, edge)
    trail = slice(size - edge, size)
    adjoint = (jnp.swapaxes(coupling_block[0], -1, -2), -jnp.swapaxes(coupling_block[1], -1, -2))

    def schur_of(incoming):
        return complex_product(complex_product(adjoint, incoming), coupling_block)

    def lead_rows_minus(values, schur, rows):
        update = newton_product(schur, rows)
        return tuple(v.at[..., lead, :].add(-u) for v, u in zip(values, update))

    applied_guess = first_step_product(blocks, guess)
    first = combine(2.0, guess, first_step_product(guess, applied_guess))
    left = part(guess, cols=lead)
    right = part(guess, rows=lead)

    applied_trail = newton_product(blocks, part(first, cols=trail))
    boundary = combine(
        2.0, part(first, trail, trail), newton_product(part(first, rows=trail), applied_trail)
    )
    applied_left = part(applied_guess, cols=lead)

    for section in range(1, space_count - 1):
        incoming = pass_boundary(boundary)
        schur = schur_of(incoming)
        mixed = first_step_product(schur, right)
        mixed_trail = part(mixed, cols=trail)
        step_trail = add(part(first, cols=trail), newton_product(left, mixed_trail))
        step_rows = add(part(first, rows=trail), newton_product(part(left, rows=trail), mixed))
        system_trail = add(applied_trail, newton_product(applied_left, mixed_trail))
        system_trail = lead_rows_minus(system_trail, schur, part(step_trail, rows=lead))
        boundary = combine(
            2.0, part(step_trail, rows=trail), newton_product(step_rows, system_trail)
        )

    applied_lead = newton_product(blocks, part(first, cols=slice(0, size - edge)))
    applied = tuple(jnp.concatenate(pair, axis=-1) for pair in zip(applied_lead, applied_trail))
    stacked_left = tuple(jnp.concatenate(pair, axis=-2) for pair in zip(left, applied_left))
    if space_count > 1:
        incoming = pass_boundary(boundary)
        schur = schur_of(incoming)
        mixed = first_step_product(schur, right)
        both = newton_product(stacked_left, mixed)
        step = add(first, part(both, rows=slice(0, size)))
        system_step = add(applied, part(both, rows=slice(size, 2 * size)))
        system_step = lead_rows_minus(system_step, schur, part(step, rows=lead))
    else:
        step = first
        system_step = applied
    return combine(2.0, step, newton_product(step, system_step))


def phonon_matrix(phonon_shift, phonon_strength, momentum_table, energies):
    momenta = momentum_table.shape[0]
    chosen = (
        momentum_table[:, :, None] == jnp.arange(momenta, dtype=jnp.int32)[None, None, :]
    ).astype(jnp.float32)
    momentum_mix = jnp.einsum("kqj,dwq->kjdw", chosen, phonon_strength, precision=HIGHEST)
    energy_rows = jnp.arange(energies, dtype=jnp.int32)
    energy_gap = energy_rows[None, :] - energy_rows[:, None]
    emission = (energy_gap[None, :, :] == -phonon_shift[:, None, None]).astype(jnp.float32)
    absorption = (energy_gap[None, :, :] == phonon_shift[:, None, None]).astype(jnp.float32)
    shift_table = jnp.stack([emission, absorption], axis=0)
    return jnp.einsum("kjdw,dwEF->kjEF", momentum_mix, shift_table, precision=HIGHEST)


def part_of(pair, index):
    return tuple(value[index : index + 1] for value in pair)


def pick_kernel(partner_ref, real_ref, imag_ref, out_ref):
    energy_count, size, _ = real_ref.shape
    chunk = out_ref.shape[2]
    atoms = size // ORB
    per_atom = partner_ref.shape[0] // atoms
    width = per_atom * ORB
    sublanes = 8
    flat = ORB * ORB
    halves = ORB // sublanes

    pick_rows = lax.broadcasted_iota(jnp.int32, (size, width), 0)
    pick_cols = lax.broadcasted_iota(jnp.int32, (size, width), 1)
    row_atom = pick_rows // ORB
    same_orbital = pick_rows % ORB == pick_cols % ORB
    grid_rows = lax.broadcasted_iota(jnp.int32, (sublanes, width), 0)
    grid_cols = lax.broadcasted_iota(jnp.int32, (sublanes, width), 1) // ORB
    diagonal = [(grid_cols - grid_rows) % per_atom == d for d in range(per_atom)]
    lane_tile = lax.broadcasted_iota(jnp.int32, (1, width), 1) // ORB

    def one_atom(atom, carry):
        target = jnp.zeros((1, width), jnp.int32)
        for j in range(per_atom):
            target = jnp.where(lane_tile == j, partner_ref[atom * per_atom + j], target)
        pick = jnp.where((row_atom == target) & same_orbital, 1.0, 0.0).astype(jnp.bfloat16)
        start = pl.multiple_of(atom * ORB, ORB)
        stripes = []
        for e in range(energy_count):
            stripes.append(real_ref[e, pl.ds(start, ORB), :])
            stripes.append(imag_ref[e, pl.ds(start, ORB), :])
        stripes = jnp.concatenate(stripes, axis=0)
        high = stripes.astype(jnp.bfloat16)
        rest = stripes - high.astype(jnp.float32)
        middle = rest.astype(jnp.bfloat16)
        low = (rest - middle.astype(jnp.float32)).astype(jnp.bfloat16)
        pieces = jnp.concatenate([high, middle, low], axis=0)
        selected = jnp.dot(pieces, pick, preferred_element_type=jnp.float32)
        rows = stripes.shape[0]
        chosen = (selected[:rows] + selected[rows : 2 * rows]) + selected[2 * rows :]
        out_start = pl.multiple_of(atom * per_atom, per_atom)
        for g in range(2 * energy_count):
            for half in range(halves):
                row = g * ORB + half * sublanes
                grid = chosen[row : row + sublanes, :]
                flipped = grid
                for d in range(1, per_atom):
                    moved = pltpu.roll(grid, (sublanes - d) % sublanes, 0)
                    moved = pltpu.roll(moved, d * ORB, 1)
                    flipped = jnp.where(diagonal[d], moved, flipped)
                lane = (g % 2) * flat + half * width
                if chunk >= per_atom:
                    out_ref[
                        out_start // chunk, g // 2, pl.ds(out_start % chunk, per_atom), pl.ds(lane, width)
                    ] = flipped
                else:
                    for q in range(per_atom // chunk):
                        out_ref[
                            atom * (per_atom // chunk) + q, g // 2, :, pl.ds(lane, width)
                        ] = flipped[q * chunk : (q + 1) * chunk]
        return carry

    lax.fori_loop(0, atoms, one_atom, 0)


def pick_tiles(green_pair, pair_index, chunks):
    energy_count = green_pair[0].shape[0]
    pair_count = pair_index.shape[0]
    partner = pair_index % ATOMS
    shape = (chunks, energy_count, pair_count // chunks, 2 * ORB * ORB)
    return pl.pallas_call(
        pick_kernel,
        out_shape=jax.ShapeDtypeStruct(shape, jnp.float32),
        in_specs=[
            pl.BlockSpec(memory_space=pltpu.SMEM),
            pl.BlockSpec(memory_space=pltpu.VMEM),
            pl.BlockSpec(memory_space=pltpu.VMEM),
        ],
        out_specs=pl.BlockSpec(memory_space=pltpu.VMEM),
    )(partner, green_pair[0], green_pair[1])


def body(
    blocks, inverse_guess, coupling, pair_index, phonon_shift, phonon_strength, momentum_table
):
    local_blocks = (blocks[:, 0, 0, 0], blocks[:, 0, 0, 1])
    local_guess = (inverse_guess[:, 0, 0, 0], inverse_guess[:, 0, 0, 1])
    coupling_block = (coupling[0, 0, 0], coupling[0, 0, 1])
    energy_count = blocks.shape[0]
    swept = [
        sweep(part_of(local_blocks, e), part_of(local_guess, e), coupling_block)
        for e in range(energy_count)
    ]
    green_pair = tuple(jnp.concatenate(values, axis=0) for values in zip(*swept))
    green_block = jnp.stack(green_pair, axis=1)
    momenta = momentum_table.shape[0]
    energy_groups = lax.axis_size("energy")
    axes = ("energy", "momentum")
    group = energy_groups * lax.axis_size("momentum")
    pair_count = pair_index.shape[1]
    width = 2 * ORB * ORB
    picked = pick_tiles(green_pair, pair_index[0], group)
    mixing = phonon_matrix(
        phonon_shift, phonon_strength, momentum_table, energy_count * energy_groups
    )
    by_pairs = lax.all_to_all(picked, axes, 0, 0, tiled=True)
    arranged = by_pairs.reshape(energy_groups, momenta, energy_count, pair_count // group, width)
    mixing_grid = mixing.reshape(
        momenta, momenta, energy_groups, energy_count, energy_groups, energy_count
    )
    summed = jnp.einsum("kjabcd,cjdpx->akbpx", mixing_grid, arranged, precision=HIGHEST)
    summed = summed.reshape(group, energy_count, pair_count // group, width)
    self_energy = lax.all_to_all(summed, axes, 0, 2, tiled=True)
    self_energy = self_energy.reshape(energy_count, 1, 1, pair_count, width)
    return (green_block[:, None, None], self_energy)


def solution(mesh):
    return jax.shard_map(
        body,
        mesh=mesh,
        in_specs=(
            P("energy", "momentum", "space", None, None, None),
            P("energy", "momentum", "space", None, None, None),
            P("momentum", "space", None, None, None),
            P("space", None),
            P(),
            P(),
            P(),
        ),
        out_specs=(
            P("energy", "momentum", "space", None, None, None),
            P("energy", "momentum", "space", None, None),
        ),
        check_vma=False,
    )
```

```python
import jax
import jax.numpy as jnp
from jax import lax
from jax.sharding import PartitionSpec as P
from jax.experimental import pallas as pl
from jax.experimental.pallas import tpu as pltpu

ORB = 16
ATOMS = 16
NEWTON = 2


HIGHEST = lax.Precision.HIGHEST
FIRST_STEP_PRECISION = lax.Precision.HIGHEST


def from_behind(shard, axis, by):
    count = lax.axis_size(axis)
    pairs = [(i, i + by) for i in range(count) if 0 <= i + by < count]
    return lax.ppermute(shard, axis, pairs)


def pass_boundary(boundary):
    moved = from_behind(jnp.stack(boundary, axis=0), "space", 1)
    return (moved[0], moved[1])


def complex_product(first_factor, second_factor, precision=HIGHEST):
    first_real, first_imag = first_factor
    second_real, second_imag = second_factor
    real_real = jnp.matmul(first_real, second_real, precision=precision)
    imag_imag = jnp.matmul(first_imag, second_imag, precision=precision)
    summed = jnp.matmul(
        first_real + first_imag, second_real + second_imag, precision=precision
    )
    return (real_real - imag_imag, summed - real_real - imag_imag)


def newton_product(first_factor, second_factor):
    return complex_product(first_factor, second_factor, HIGHEST)


def first_step_product(first_factor, second_factor):
    return complex_product(first_factor, second_factor, FIRST_STEP_PRECISION)


def part(pair, rows=slice(None), cols=slice(None)):
    return tuple(value[..., rows, cols] for value in pair)


def combine(first_weight, first, second):
    return tuple(first_weight * a - b for a, b in zip(first, second))


def add(first, second):
    return tuple(a + b for a, b in zip(first, second))


def sweep(blocks, guess, coupling_block):
    space_count = lax.axis_size("space")
    size = blocks[0].shape[-1]
    edge = coupling_block[0].shape[-1]
    lead = slice(0, edge)
    trail = slice(size - edge, size)
    adjoint = (jnp.swapaxes(coupling_block[0], -1, -2), -jnp.swapaxes(coupling_block[1], -1, -2))

    def schur_of(incoming):
        return complex_product(complex_product(adjoint, incoming), coupling_block)

    def lead_rows_minus(values, schur, rows):
        update = newton_product(schur, rows)
        return tuple(
            jnp.concatenate([v[..., lead, :] - u, v[..., edge:, :]], axis=-2)
            for v, u in zip(values, update)
        )

    applied_guess = first_step_product(blocks, guess)
    first = combine(2.0, guess, first_step_product(guess, applied_guess))
    left = part(guess, cols=lead)
    right = part(guess, rows=lead)

    applied_trail = newton_product(blocks, part(first, cols=trail))
    boundary = combine(
        2.0, part(first, trail, trail), newton_product(part(first, rows=trail), applied_trail)
    )
    applied_left = part(applied_guess, cols=lead)

    for section in range(1, space_count - 1):
        incoming = pass_boundary(boundary)
        schur = schur_of(incoming)
        mixed = first_step_product(schur, right)
        mixed_trail = part(mixed, cols=trail)
        step_trail = add(part(first, cols=trail), newton_product(left, mixed_trail))
        step_rows = add(part(first, rows=trail), newton_product(part(left, rows=trail), mixed))
        system_trail = add(applied_trail, newton_product(applied_left, mixed_trail))
        system_trail = lead_rows_minus(system_trail, schur, part(step_trail, rows=lead))
        boundary = combine(
            2.0, part(step_trail, rows=trail), newton_product(step_rows, system_trail)
        )

    applied_lead = newton_product(blocks, part(first, cols=slice(0, size - edge)))
    applied = tuple(jnp.concatenate(pair, axis=-1) for pair in zip(applied_lead, applied_trail))
    stacked_left = tuple(jnp.concatenate(pair, axis=-2) for pair in zip(left, applied_left))
    if space_count > 1:
        incoming = pass_boundary(boundary)
        schur = schur_of(incoming)
        mixed = first_step_product(schur, right)
        both = newton_product(stacked_left, mixed)
        step = add(first, part(both, rows=slice(0, size)))
        system_step = add(applied, part(both, rows=slice(size, 2 * size)))
        system_step = lead_rows_minus(system_step, schur, part(step, rows=lead))
    else:
        step = first
        system_step = applied
    return combine(2.0, step, newton_product(step, system_step))


def phonon_matrix(phonon_shift, phonon_strength, momentum_table, energies):
    momenta = momentum_table.shape[0]
    chosen = (
        momentum_table[:, :, None] == jnp.arange(momenta, dtype=jnp.int32)[None, None, :]
    ).astype(jnp.float32)
    momentum_mix = jnp.einsum("kqj,dwq->kjdw", chosen, phonon_strength, precision=HIGHEST)
    energy_rows = jnp.arange(energies, dtype=jnp.int32)
    energy_gap = energy_rows[None, :] - energy_rows[:, None]
    emission = (energy_gap[None, :, :] == -phonon_shift[:, None, None]).astype(jnp.float32)
    absorption = (energy_gap[None, :, :] == phonon_shift[:, None, None]).astype(jnp.float32)
    shift_table = jnp.stack([emission, absorption], axis=0)
    return jnp.einsum("kjdw,dwEF->kjEF", momentum_mix, shift_table, precision=HIGHEST)


def pick_kernel(partner_ref, real_ref, imag_ref, out_ref):
    energy_count, size, _ = real_ref.shape
    chunk = out_ref.shape[2]
    atoms = size // ORB
    per_atom = partner_ref.shape[0] // atoms
    width = per_atom * ORB
    sublanes = 8
    flat = ORB * ORB
    halves = ORB // sublanes

    pick_rows = lax.broadcasted_iota(jnp.int32, (size, width), 0)
    pick_cols = lax.broadcasted_iota(jnp.int32, (size, width), 1)
    row_atom = pick_rows // ORB
    same_orbital = pick_rows % ORB == pick_cols % ORB
    grid_rows = lax.broadcasted_iota(jnp.int32, (sublanes, width), 0)
    grid_cols = lax.broadcasted_iota(jnp.int32, (sublanes, width), 1) // ORB
    diagonal = [(grid_cols - grid_rows) % per_atom == d for d in range(per_atom)]
    lane_tile = lax.broadcasted_iota(jnp.int32, (1, width), 1) // ORB

    def one_atom(atom, carry):
        target = jnp.zeros((1, width), jnp.int32)
        for j in range(per_atom):
            target = jnp.where(lane_tile == j, partner_ref[atom * per_atom + j], target)
        pick = jnp.where((row_atom == target) & same_orbital, 1.0, 0.0).astype(jnp.bfloat16)
        start = pl.multiple_of(atom * ORB, ORB)
        stripes = []
        for e in range(energy_count):
            stripes.append(real_ref[e, pl.ds(start, ORB), :])
            stripes.append(imag_ref[e, pl.ds(start, ORB), :])
        stripes = jnp.concatenate(stripes, axis=0)
        high = stripes.astype(jnp.bfloat16)
        rest = stripes - high.astype(jnp.float32)
        middle = rest.astype(jnp.bfloat16)
        low = (rest - middle.astype(jnp.float32)).astype(jnp.bfloat16)
        pieces = jnp.concatenate([high, middle, low], axis=0)
        selected = jnp.dot(pieces, pick, preferred_element_type=jnp.float32)
        rows = stripes.shape[0]
        chosen = (selected[:rows] + selected[rows : 2 * rows]) + selected[2 * rows :]
        out_start = pl.multiple_of(atom * per_atom, per_atom)
        for g in range(2 * energy_count):
            for half in range(halves):
                row = g * ORB + half * sublanes
                grid = chosen[row : row + sublanes, :]
                flipped = grid
                for d in range(1, per_atom):
                    moved = pltpu.roll(grid, (sublanes - d) % sublanes, 0)
                    moved = pltpu.roll(moved, d * ORB, 1)
                    flipped = jnp.where(diagonal[d], moved, flipped)
                lane = (g % 2) * flat + half * width
                if chunk >= per_atom:
                    out_ref[
                        out_start // chunk, g // 2, pl.ds(out_start % chunk, per_atom), pl.ds(lane, width)
                    ] = flipped
                else:
                    for q in range(per_atom // chunk):
                        out_ref[
                            atom * (per_atom // chunk) + q, g // 2, :, pl.ds(lane, width)
                        ] = flipped[q * chunk : (q + 1) * chunk]
        return carry

    lax.fori_loop(0, atoms, one_atom, 0)


def pick_tiles(green_pair, pair_index, chunks):
    energy_count = green_pair[0].shape[0]
    pair_count = pair_index.shape[0]
    partner = pair_index % ATOMS
    shape = (chunks, energy_count, pair_count // chunks, 2 * ORB * ORB)
    return pl.pallas_call(
        pick_kernel,
        out_shape=jax.ShapeDtypeStruct(shape, jnp.float32),
        in_specs=[
            pl.BlockSpec(memory_space=pltpu.SMEM),
            pl.BlockSpec(memory_space=pltpu.VMEM),
            pl.BlockSpec(memory_space=pltpu.VMEM),
        ],
        out_specs=pl.BlockSpec(memory_space=pltpu.VMEM),
    )(partner, green_pair[0], green_pair[1])


def body(
    blocks, inverse_guess, coupling, pair_index, phonon_shift, phonon_strength, momentum_table
):
    local_blocks = (blocks[:, 0, 0, 0], blocks[:, 0, 0, 1])
    local_guess = (inverse_guess[:, 0, 0, 0], inverse_guess[:, 0, 0, 1])
    coupling_block = (coupling[0, 0, 0], coupling[0, 0, 1])
    energy_count = blocks.shape[0]
    green_pair = sweep(local_blocks, local_guess, coupling_block)
    green_block = jnp.stack(green_pair, axis=1)
    momenta = momentum_table.shape[0]
    energy_groups = lax.axis_size("energy")
    axes = ("energy", "momentum")
    group = energy_groups * lax.axis_size("momentum")
    pair_count = pair_index.shape[1]
    width = 2 * ORB * ORB
    picked = pick_tiles(green_pair, pair_index[0], group)
    mixing = phonon_matrix(
        phonon_shift, phonon_strength, momentum_table, energy_count * energy_groups
    )
    by_pairs = lax.all_to_all(picked, axes, 0, 0, tiled=True)
    arranged = by_pairs.reshape(energy_groups, momenta, energy_count, pair_count // group, width)
    mixing_grid = mixing.reshape(
        momenta, momenta, energy_groups, energy_count, energy_groups, energy_count
    )
    summed = jnp.einsum("kjabcd,cjdpx->akbpx", mixing_grid, arranged, precision=HIGHEST)
    summed = summed.reshape(group, energy_count, pair_count // group, width)
    self_energy = lax.all_to_all(summed, axes, 0, 2, tiled=True)
    self_energy = self_energy.reshape(energy_count, 1, 1, pair_count, width)
    return (green_block[:, None, None], self_energy)


def solution(mesh):
    return jax.shard_map(
        body,
        mesh=mesh,
        in_specs=(
            P("energy", "momentum", "space", None, None, None),
            P("energy", "momentum", "space", None, None, None),
            P("momentum", "space", None, None, None),
            P("space", None),
            P(),
            P(),
            P(),
        ),
        out_specs=(
            P("energy", "momentum", "space", None, None, None),
            P("energy", "momentum", "space", None, None),
        ),
        check_vma=False,
    )
```
